512 devices in a mesh: ctx: 64 (over z, y_lo, core), tp: 8 (over y_hi, x).
Axes of the slice: x: 4, y: 8 (y_hi: 2, y_lo: 4; y = y_hi * 4 + y_lo), z: 8, core: 2. Of those that a mesh axis runs over, the one named last changes fastest.
Arguments:
- qkv: bfloat16 [8192, 3, 8192], P('ctx', None, 'tp'), may hold values from -2048 to 2048
- taps: float32 [7, 3, 8192], P(None, None, 'tp'), may hold values from -2 to 2
- rate: float32 [512, 16], P('tp'), may hold values from 0 to 1
- angle: float32 [512, 16], P('tp'), may hold values from -0.5 to 0.5
- residue: float32 [2, 512, 16], P(None, 'tp'), may hold values from -3 to 3
- skip: float32 [8192], P('tp'), may hold values from 0.5 to 1.5
- gain: float32 [8192], P('tp'), may hold values from 0.25 to 1.75
- lengths: int32 [4], replicated, may hold values from 1 to 4096, 8192 in all
Outputs:
- mixed: bfloat16 [8192, 8192], P('ctx', 'tp')
The draws below stay inside these ranges and needn't reach their ends.
Inputs may be any that keep to these rules, and one draw needn't show every extreme that they name: `lengths`: they sum to 8192.
All inputs are finite; a program needn't handle non-finite values.
Results may differ from the reference program's by a relative error of at most 0.001.
Values may be sent and summed in bfloat16 or wider, within the bound.
No kernel may reach another device: no remote copies, remote signals or barrier semaphores. Data moves between devices by JAX's collectives and lax.ppermute only.
A program may use at most 128 MiB of HBM per device.

```python
import math
import jax
import jax.numpy as jnp
import numpy as np
from jax import lax

D = 8192
GSIZE = 16
MODES = 16
SHORT = 7
SPAN = 128
GENOMES = 4
TOKENS = 8192
GROUPS = 512
N_TP = 8


def pole_rates(key):
    pick_key, fast_key, slow_key = jax.random.split(jax.random.fold_in(key, 11), 3)
    slow_share = 0.5
    slow_mask = jax.random.uniform(pick_key, (GROUPS, MODES)) < slow_share
    fast_rate = jnp.exp(jax.random.uniform(fast_key, (GROUPS, MODES), minval=math.log(0.05), maxval=math.log(0.15)))
    slow_rate = jnp.exp(jax.random.uniform(slow_key, (GROUPS, MODES), minval=math.log(0.1), maxval=math.log(2.0))) / TOKENS
    return jnp.where(slow_mask, slow_rate, fast_rate).astype(jnp.float32)


def draw_rate(key, part):
    return pole_rates(key)


def draw_residue(key, part):
    rates = pole_rates(key)
    noise_key = jax.random.fold_in(key, 23)
    noise = jnp.clip(jax.random.normal(noise_key, (2, GROUPS, MODES)), -4.0, 4.0)
    return (noise * jnp.sqrt(2.0 * rates)[None]).astype(jnp.float32)


def draw_qkv(key, part):
    base_key, column_key, row_key = jax.random.split(jax.random.fold_in(key, 37), 3)
    ramp = 3.0 ** (jnp.arange(D).astype(jnp.float32) / (D - 1))
    columns = 10.0 ** jax.random.uniform(column_key, (D,)) * ramp
    rows_scale = 10.0 ** jax.random.uniform(row_key, (TOKENS,))
    noise = jnp.clip(jax.random.normal(base_key, (TOKENS, 3, D)), -4.0, 4.0)
    stream_q = (jnp.arange(3) == 0)[None, :, None]
    scaling = jnp.where(stream_q, rows_scale[:, None, None] * columns[None, None, :], 1.0)
    return (noise * scaling).astype(jnp.bfloat16)


def steps_of(stream_key, extent, cuts, least, high):
    level = 1.0
    for dim, parts in cuts:
        steps = jax.random.uniform(jax.random.fold_in(jax.random.fold_in(stream_key, 6), dim), (parts,), jnp.float32, least / len(cuts), high / len(cuts))
        level = level * jnp.repeat(jnp.exp(steps), extent[dim] // parts).reshape((-1,) + (1,) * (len(extent) - 1 - dim))
    return level


def profile(number_of, total, bound, lean):
    weights = [(1 << 20) // math.isqrt(rank ** lean) + 1 for rank in range(2, number_of + 1)]
    surplus, given = total - bound - (number_of - 1), [1] * (number_of - 1)
    while surplus > 0:
        free = [i for i in range(number_of - 1) if given[i] < bound]
        whole, left = sum([weights[i] for i in free]), surplus
        for i in free:
            more = min(bound - given[i], max(1, left * weights[i] // whole), surplus)
            given[i] = given[i] + more
            surplus = surplus - more
    return np.array([bound] + given)


def uneven(key, amount, total, bound, skew):
    if amount == 2:
        one = jax.random.randint(key, (), max(1, total - bound), min(bound, total - 1) + 1)
        return jnp.stack([one, total - one])
    sizes = jnp.asarray(profile(amount, total, bound, skew), jnp.int32)
    pairs = (amount - 1) // 2
    source_of, sink = sizes[1:1 + 2 * pairs:2], sizes[2:2 + 2 * pairs:2]
    room = jnp.minimum(source_of - 1, bound - sink)
    passed = jax.random.randint(jax.random.fold_in(key, 1), (pairs,), 0, 1 << 20) % (room + 1)
    sizes = sizes.at[1:1 + 2 * pairs:2].set(source_of - passed).at[2:2 + 2 * pairs:2].set(sink + passed)
    return sizes[jax.random.permutation(jax.random.fold_in(key, 2), amount)]


def scatter_about(rng, extent, scale, limit, cuts=(), kind=jnp.bfloat16):
    level = steps_of(rng, extent, cuts, -0.22, 0.18) if cuts else 1.0
    drawn = jax.random.normal(rng, extent, jnp.float32) * scale * level
    return jnp.minimum(jnp.maximum(drawn, -limit), limit).astype(kind)


def setup_inputs(seed: int = 0) -> dict:
    splits = jax.random.split(jax.random.key(seed), 9)
    return {
        "qkv": draw_qkv(jax.random.fold_in(splits[8], 71), 0),
        "taps": scatter_about(splits[1], (SHORT, 3, D), SHORT ** -0.5, 2.0, ((2, 8),), jnp.float32),
        "rate": draw_rate(jax.random.fold_in(splits[8], 71), 0),
        "angle": jnp.clip(jax.random.uniform(splits[3], (GROUPS, MODES), jnp.float32, -0.5, 0.5) * steps_of(splits[3], (GROUPS, MODES), ((0, 8),), -0.4, 0.0), -0.5, 0.5),
        "residue": draw_residue(jax.random.fold_in(splits[8], 71), 0),
        "skip": jnp.clip(0.5 + 1.0 * jax.random.uniform(splits[5], (D,), jnp.float32) ** steps_of(splits[5], (D,), ((0, 8),), -0.2, 0.2), 0.5, 1.5),
        "gain": jnp.clip(1.0 + 0.15 * jax.random.normal(splits[6], (D,), jnp.float32), 0.25, 1.75),
        "lengths": uneven(splits[7], GENOMES, TOKENS, TOKENS // 2, 1).astype(jnp.int32),
    }


HIGHEST = lax.Precision.HIGHEST
EPSILON = 1e-06

def genome_begin(lengths, positions):
    lengths = lengths.astype(jnp.int32)
    ending = jnp.cumsum(lengths).astype(jnp.int32)
    starting = ending - lengths
    reached = starting[None, :] <= positions[:, None]
    return lax.optimization_barrier(jnp.max(jnp.where(reached, starting[None, :], 0), axis=1)).astype(jnp.int32)

def toeplitz(response):
    group_count, block = response.shape
    folded = jnp.concatenate([response[:, :1], jnp.zeros((group_count, block), response.dtype), response[:, :0:-1]], axis=1)
    tiled = jnp.tile(folded, (1, block))[:, :block * (2 * block - 1)]
    return tiled.reshape(group_count, block, 2 * block - 1)[:, :, :block]

def pole_tables(rate, angle, residue, block):
    counter = jnp.arange(block + 1).astype(jnp.float32)
    magnitude = jnp.exp(-rate[:, :, None] * counter)
    power_re = magnitude * jnp.cos(angle[:, :, None] * counter)
    power_im = magnitude * jnp.sin(angle[:, :, None] * counter)
    resid_re = residue[0][:, :, None]
    resid_im = residue[1][:, :, None]
    response = lax.optimization_barrier(jnp.sum(resid_re * power_re[:, :, :block] - resid_im * power_im[:, :, :block], axis=1))
    enter_re = resid_re * power_re[:, :, 1:] - resid_im * power_im[:, :, 1:]
    enter_im = resid_re * power_im[:, :, 1:] + resid_im * power_re[:, :, 1:]
    entering = jnp.stack([enter_re, -enter_im])
    leaving = jnp.stack([power_re[:, :, block - 1::-1], power_im[:, :, block - 1::-1]])
    stepping = jnp.stack([power_re[:, :, block].T, power_im[:, :, block].T])
    return (toeplitz(response), entering, leaving, stepping)

def complex_times(factor_one, factor_two):
    return jnp.stack([factor_one[0] * factor_two[0] - factor_one[1] * factor_two[1], factor_one[0] * factor_two[1] + factor_one[1] * factor_two[0]])

def block_terms(tables, values, block_positions, block_starts):
    matrix_table, entering, leaving, stepping = tables
    same_genome = (block_positions[None, :] >= block_starts[:, None]).astype(jnp.float32)
    inside = jnp.einsum('gts,sgc->tgc', matrix_table * same_genome[None], values, precision=HIGHEST)
    tail_mask = (block_positions >= block_starts[-1]).astype(jnp.float32)
    fresh_state = jnp.einsum('rgns,sgc->rngc', leaving * tail_mask, values, precision=HIGHEST)
    return (inside, fresh_state)

def carried(entering, carry_state):
    return jnp.einsum('rgnt,rngc->tgc', entering, carry_state, precision=HIGHEST)

def short_filter(padded, taps_part, positions, genome_start):
    lead = taps_part.shape[0] - 1
    row_count = positions.shape[0]
    result = jnp.zeros((row_count,) + padded.shape[1:], jnp.float32)
    for offset in range(taps_part.shape[0]):
        keep_tap = (positions - offset >= genome_start)[:, None, None]
        window = padded[lead - offset:lead - offset + row_count].astype(jnp.float32)
        result = result + jnp.where(keep_tap, taps_part[offset][None] * window, 0.0)
    return result

def mixer_block(qkv_part, taps_part, rate_part, angle_part, residue_part, skip_part, positions, genome_start):
    channels = qkv_part.shape[2]
    group_count = rate_part.shape[0]
    padded = jnp.concatenate([jnp.zeros((SHORT - 1, 3, channels), jnp.bfloat16), qkv_part], axis=0)
    filtered = short_filter(padded, taps_part, positions, genome_start)
    product = filtered[:, 1] * filtered[:, 2]
    tables = pole_tables(rate_part, angle_part, residue_part, SPAN)
    block_count = TOKENS // SPAN
    values = product.reshape(block_count, SPAN, group_count, GSIZE)

    def advance_block(carry_state, inputs):
        piece_values, block_positions, block_starts = inputs
        inside, fresh_state = block_terms(tables, piece_values, block_positions, block_starts)
        entered = (block_starts < block_positions[0])[:, None, None]
        output = inside + jnp.where(entered, carried(tables[1], carry_state), 0.0)
        keep_state = block_starts[-1] < block_positions[0]
        carry_state = jnp.where(keep_state, complex_times(tables[3][:, :, :, None], carry_state), 0.0) + fresh_state
        return (carry_state, output)
    initial = jnp.zeros((2, MODES, group_count, GSIZE), jnp.float32)
    final_state, outputs = lax.scan(advance_block, initial, (values, positions.reshape(block_count, SPAN), genome_start.reshape(block_count, SPAN)))
    long_part = outputs.reshape(TOKENS, channels)
    return filtered[:, 0] * (long_part + skip_part[None] * product)

def reference(qkv, taps, rate, angle, residue, skip, gain, lengths):
    channels = D // N_TP
    group_width = channels // GSIZE
    positions = jnp.arange(TOKENS).astype(jnp.int32)
    genome_start = genome_begin(lengths, positions)

    def one_block(block_index):
        channel_start = block_index * channels
        group_start = block_index * group_width
        return mixer_block(lax.dynamic_slice_in_dim(qkv, channel_start, channels, 2), lax.dynamic_slice_in_dim(taps, channel_start, channels, 2), lax.dynamic_slice_in_dim(rate, group_start, group_width, 0), lax.dynamic_slice_in_dim(angle, group_start, group_width, 0), lax.dynamic_slice_in_dim(residue, group_start, group_width, 1), lax.dynamic_slice_in_dim(skip, channel_start, channels, 0), positions, genome_start)
    gated_rows = lax.map(one_block, jnp.arange(N_TP).astype(jnp.int32))
    gated_rows = jnp.transpose(gated_rows, (1, 0, 2)).reshape(TOKENS, D)
    squares = lax.optimization_barrier(jnp.sum(gated_rows * gated_rows, axis=1))
    root_mean = jnp.sqrt(squares / D + EPSILON)
    return (gated_rows / root_mean[:, None] * gain[None]).astype(jnp.bfloat16)
```

```python
import jax
import jax.numpy as jnp
from jax import lax
from jax.sharding import PartitionSpec as P

D = 8192
SPAN = 128


HIGHEST = lax.Precision.HIGHEST
EPSILON = 1e-06


def passed_along(block, axis, distance):
    devices = range(lax.axis_size(axis))
    route = [(i - distance, i) for i in devices if i - distance in devices]
    return lax.ppermute(block, axis, route)


def genome_begin(lengths, positions):
    ending = jnp.cumsum(lengths)
    starting = ending - lengths
    reached = starting[None, :] <= positions[:, None]
    return jnp.max(jnp.where(reached, starting[None, :], 0), axis=1)


def toeplitz(response):
    group_count, block = response.shape
    folded = jnp.concatenate(
        [response[:, :1], jnp.zeros((group_count, block), response.dtype), response[:, :0:-1]],
        axis=1,
    )
    tiled = jnp.tile(folded, (1, block))[:, : block * (2 * block - 1)]
    return tiled.reshape(group_count, block, 2 * block - 1)[:, :, :block]


def pole_tables(rate, angle, residue, block):
    counter = jnp.arange(block + 1).astype(jnp.float32)
    magnitude = jnp.exp(-rate[:, :, None] * counter)
    power_re = magnitude * jnp.cos(angle[:, :, None] * counter)
    power_im = magnitude * jnp.sin(angle[:, :, None] * counter)
    resid_re = residue[0][:, :, None]
    resid_im = residue[1][:, :, None]
    response = jnp.sum(
        resid_re * power_re[:, :, :block] - resid_im * power_im[:, :, :block], axis=1
    )
    enter_re = resid_re * power_re[:, :, 1:] - resid_im * power_im[:, :, 1:]
    enter_im = resid_re * power_im[:, :, 1:] + resid_im * power_re[:, :, 1:]
    entering = jnp.stack([enter_re, -enter_im])
    leaving = jnp.stack([power_re[:, :, block - 1 :: -1], power_im[:, :, block - 1 :: -1]])
    stepping = jnp.stack([power_re[:, :, block].T, power_im[:, :, block].T])
    return (toeplitz(response), entering, leaving, stepping)


def complex_times(factor_one, factor_two):
    return jnp.stack(
        [
            factor_one[0] * factor_two[0] - factor_one[1] * factor_two[1],
            factor_one[0] * factor_two[1] + factor_one[1] * factor_two[0],
        ]
    )


def block_terms(tables, columns, block_positions, block_starts):
    matrix_table, entering, leaving, stepping = tables
    same_genome = (block_positions[None, :] >= block_starts[:, None]).astype(jnp.float32)
    inside = jnp.einsum(
        "gts,gis->git", matrix_table * same_genome[None], columns, precision=HIGHEST
    )
    tail_mask = (block_positions >= block_starts[-1]).astype(jnp.float32)
    fresh_state = jnp.einsum("rgns,gis->rngi", leaving * tail_mask, columns, precision=HIGHEST)
    return (inside, fresh_state)


def carried(entering, carry_state):
    return jnp.einsum("rgnt,rngi->git", entering, carry_state, precision=HIGHEST)


def short_filter(padded, taps_part, positions, genome_start):
    lead = taps_part.shape[0] - 1
    row_count = positions.shape[0]
    result = jnp.zeros((row_count,) + padded.shape[1:], jnp.float32)
    for offset in range(taps_part.shape[0]):
        keep_tap = (positions - offset >= genome_start)[:, None, None]
        window = padded[lead - offset : lead - offset + row_count].astype(jnp.float32)
        result = result + jnp.where(keep_tap, taps_part[offset][None] * window, 0.0)
    return result


def on_device(qkv, taps, rate, angle, residue, skip, gain, lengths):
    tok_rows = qkv.shape[0]
    channels = qkv.shape[2]
    group_count = rate.shape[0]
    group_width = channels // group_count
    mode_count = rate.shape[1]
    reach = taps.shape[0]
    span_count = tok_rows // SPAN
    device = lax.axis_index("ctx")
    anchor = device * tok_rows
    positions = anchor + jnp.arange(tok_rows, dtype=jnp.int32)
    genome_start = genome_begin(lengths, positions)
    before = passed_along(qkv[tok_rows - (reach - 1) :], "ctx", 1)
    padded = jnp.concatenate([before, qkv], axis=0)
    filtered = short_filter(padded, taps, positions, genome_start)
    product = filtered[:, 1] * filtered[:, 2]
    tables = pole_tables(rate, angle, residue, SPAN)
    stepping = tables[3]
    values = jnp.transpose(
        product.reshape(span_count, SPAN, group_count, group_width), (0, 2, 3, 1)
    )
    span_pos = positions.reshape(span_count, SPAN)
    span_begin = genome_start.reshape(span_count, SPAN)
    summary = jnp.zeros((2, mode_count, group_count, group_width), jnp.float32)
    freshes = []
    keepers = []
    span_index = 0
    inside, fresh_state = block_terms(
        tables, values[span_index], span_pos[span_index], span_begin[span_index]
    )
    keep_state = span_begin[span_index, -1] < span_pos[span_index, 0]
    summary = jnp.where(keep_state, complex_times(stepping[..., None], summary), 0.0) + fresh_state
    insides = [inside]
    freshes.append(fresh_state)
    keepers.append(keep_state)
    device_count = lax.axis_size("ctx")
    starting = jnp.cumsum(lengths) - lengths

    def unbroken(first_row, last_row):
        hit = (starting >= first_row) & (starting <= last_row)
        return jnp.logical_not(jnp.any(hit))

    def widen(factor):
        return jnp.repeat(factor, group_width, axis=2)

    running = passed_along(summary.reshape(2, mode_count, channels), "ctx", 1)
    power = stepping
    distance = 1
    while distance < device_count:
        earlier = passed_along(running, "ctx", distance)
        alive = unbroken(anchor - distance * tok_rows, anchor - 1)
        factor = widen(power) * alive.astype(jnp.float32)
        running = running + complex_times(factor, earlier)
        power = complex_times(power, power)
        distance = distance * 2
    incoming = running.reshape(2, mode_count, group_count, group_width)
    span_index = 0
    entered = (span_begin[span_index] < span_pos[span_index, 0])[None, None, :]
    outputs = [insides[span_index] + jnp.where(entered, carried(tables[1], incoming), 0.0)]
    stacked = jnp.stack(outputs, axis=0)
    long_part = jnp.transpose(stacked, (0, 3, 1, 2)).reshape(tok_rows, channels)
    gated_rows = filtered[:, 0] * (long_part + skip[None] * product)
    squares = lax.psum(jnp.sum(gated_rows * gated_rows, axis=1), "tp")
    root_mean = jnp.sqrt(squares / D + EPSILON)
    return (gated_rows / root_mean[:, None] * gain[None]).astype(jnp.bfloat16)


def solution(mesh):
    return jax.shard_map(
        on_device,
        mesh=mesh,
        in_specs=(
            P("ctx", None, "tp"),
            P(None, None, "tp"),
            P("tp", None),
            P("tp", None),
            P(None, "tp", None),
            P("tp"),
            P("tp"),
            P(),
        ),
        out_specs=P("ctx", "tp"),
        check_vma=False,
    )
```

```python
import jax
import jax.numpy as jnp
from jax import lax
from jax.sharding import PartitionSpec as P

D = 8192
SPAN = 128
GENOME_MAX = 4096


HIGHEST = lax.Precision.HIGHEST
EPSILON = 1e-06


def passed_along(block, axis, distance):
    devices = range(lax.axis_size(axis))
    route = [(i - distance, i) for i in devices if i - distance in devices]
    return lax.ppermute(block, axis, route)


def genome_begin(lengths, positions):
    ending = jnp.cumsum(lengths)
    starting = ending - lengths
    reached = starting[None, :] <= positions[:, None]
    return jnp.max(jnp.where(reached, starting[None, :], 0), axis=1)


def toeplitz(response):
    group_count, block = response.shape
    folded = jnp.concatenate(
        [response[:, :1], jnp.zeros((group_count, block), response.dtype), response[:, :0:-1]],
        axis=1,
    )
    tiled = jnp.tile(folded, (1, block))[:, : block * (2 * block - 1)]
    return tiled.reshape(group_count, block, 2 * block - 1)[:, :, :block]


def pole_tables(rate, angle, residue, block):
    counter = jnp.arange(block + 1).astype(jnp.float32)
    magnitude = jnp.exp(-rate[:, :, None] * counter)
    power_re = magnitude * jnp.cos(angle[:, :, None] * counter)
    power_im = magnitude * jnp.sin(angle[:, :, None] * counter)
    resid_re = residue[0][:, :, None]
    resid_im = residue[1][:, :, None]
    response = jnp.sum(
        resid_re * power_re[:, :, :block] - resid_im * power_im[:, :, :block], axis=1
    )
    enter_re = resid_re * power_re[:, :, 1:] - resid_im * power_im[:, :, 1:]
    enter_im = resid_re * power_im[:, :, 1:] + resid_im * power_re[:, :, 1:]
    entering = jnp.stack([enter_re, -enter_im])
    leaving = jnp.stack([power_re[:, :, block - 1 :: -1], power_im[:, :, block - 1 :: -1]])
    stepping = jnp.stack([power_re[:, :, block].T, power_im[:, :, block].T])
    return (toeplitz(response), entering, leaving, stepping)


def complex_times(factor_one, factor_two):
    return jnp.stack(
        [
            factor_one[0] * factor_two[0] - factor_one[1] * factor_two[1],
            factor_one[0] * factor_two[1] + factor_one[1] * factor_two[0],
        ]
    )


def block_terms(tables, columns, block_positions, block_starts):
    matrix_table, entering, leaving, stepping = tables
    same_genome = (block_positions[None, :] >= block_starts[:, None]).astype(jnp.float32)
    inside = jnp.einsum(
        "gts,gis->git", matrix_table * same_genome[None], columns, precision=HIGHEST
    )
    tail_mask = (block_positions >= block_starts[-1]).astype(jnp.float32)
    fresh_state = jnp.einsum("rgns,gis->rngi", leaving * tail_mask, columns, precision=HIGHEST)
    return (inside, fresh_state)


def carried(entering, carry_state):
    return jnp.einsum("rgnt,rngi->git", entering, carry_state, precision=HIGHEST)


def short_filter(padded, taps_part, positions, genome_start):
    lead = taps_part.shape[0] - 1
    row_count = positions.shape[0]
    result = jnp.zeros((row_count,) + padded.shape[1:], jnp.float32)
    for offset in range(taps_part.shape[0]):
        keep_tap = (positions - offset >= genome_start)[:, None, None]
        window = padded[lead - offset : lead - offset + row_count].astype(jnp.float32)
        result = result + jnp.where(keep_tap, taps_part[offset][None] * window, 0.0)
    return result


def on_device(qkv, taps, rate, angle, residue, skip, gain, lengths):
    tok_rows = qkv.shape[0]
    channels = qkv.shape[2]
    group_count = rate.shape[0]
    group_width = channels // group_count
    mode_count = rate.shape[1]
    reach = taps.shape[0]
    span_count = tok_rows // SPAN
    device = lax.axis_index("ctx")
    anchor = device * tok_rows
    positions = anchor + jnp.arange(tok_rows, dtype=jnp.int32)
    genome_start = genome_begin(lengths, positions)
    before = passed_along(qkv[tok_rows - (reach - 1) :], "ctx", 1)
    padded = jnp.concatenate([before, qkv], axis=0)
    filtered = short_filter(padded, taps, positions, genome_start)
    product = filtered[:, 1] * filtered[:, 2]
    tables = pole_tables(rate, angle, residue, SPAN)
    stepping = tables[3]
    values = jnp.transpose(
        product.reshape(span_count, SPAN, group_count, group_width), (0, 2, 3, 1)
    )
    span_pos = positions.reshape(span_count, SPAN)
    span_begin = genome_start.reshape(span_count, SPAN)
    summary = jnp.zeros((2, mode_count, group_count, group_width), jnp.float32)
    freshes = []
    keepers = []
    span_index = 0
    inside, fresh_state = block_terms(
        tables, values[span_index], span_pos[span_index], span_begin[span_index]
    )
    keep_state = span_begin[span_index, -1] < span_pos[span_index, 0]
    summary = jnp.where(keep_state, complex_times(stepping[..., None], summary), 0.0) + fresh_state
    insides = [inside]
    freshes.append(fresh_state)
    keepers.append(keep_state)
    starting = jnp.cumsum(lengths) - lengths
    reach_rows = GENOME_MAX - 1
    reach = -(-reach_rows // tok_rows)

    def unbroken(first_row, last_row):
        hit = (starting >= first_row) & (starting <= last_row)
        return jnp.logical_not(jnp.any(hit)).astype(jnp.float32)

    def widen(factor):
        return jnp.repeat(factor, group_width, axis=2)

    powers = {1: stepping}

    def power_of(count):
        if count not in powers:
            half = power_of(count // 2)
            whole = complex_times(half, half)
            if count % 2:
                whole = complex_times(whole, stepping)
            powers[count] = whole
        return powers[count]

    fresh = summary.reshape(2, mode_count, channels)
    running = passed_along(fresh, "ctx", 1)
    for distance in range(2, min(4, reach) + 1):
        earlier = passed_along(fresh, "ctx", distance)
        alive = unbroken(anchor - (distance - 1) * tok_rows, anchor - 1)
        running = running + complex_times(widen(power_of(distance - 1)) * alive, earlier)
    covered = min(4, reach)
    while covered < reach:
        stride = covered
        width = min(4, -(-reach // stride))
        total = running
        for hop in range(1, width):
            distance = hop * stride
            earlier = passed_along(running, "ctx", distance)
            alive = unbroken(anchor - distance * tok_rows, anchor - 1)
            total = total + complex_times(widen(power_of(distance)) * alive, earlier)
        running = total
        covered = stride * width
    incoming = running.reshape(2, mode_count, group_count, group_width)
    span_index = 0
    entered = (span_begin[span_index] < span_pos[span_index, 0])[None, None, :]
    outputs = [insides[span_index] + jnp.where(entered, carried(tables[1], incoming), 0.0)]
    stacked = jnp.stack(outputs, axis=0)
    long_part = jnp.transpose(stacked, (0, 3, 1, 2)).reshape(tok_rows, channels)
    gated_rows = filtered[:, 0] * (long_part + skip[None] * product)
    squares = lax.psum(jnp.sum(gated_rows * gated_rows, axis=1), "tp")
    root_mean = jnp.sqrt(squares / D + EPSILON)
    return (gated_rows / root_mean[:, None] * gain[None]).astype(jnp.bfloat16)


def solution(mesh):
    return jax.shard_map(
        on_device,
        mesh=mesh,
        in_specs=(
            P("ctx", None, "tp"),
            P(None, None, "tp"),
            P("tp", None),
            P("tp", None),
            P(None, "tp", None),
            P("tp"),
            P("tp"),
            P(),
        ),
        out_specs=P("ctx", "tp"),
        check_vma=False,
    )
```

```python
import jax
import jax.numpy as jnp
from jax import lax
from jax.sharding import PartitionSpec as P

D = 8192
SPAN = 128
GENOME_MAX = 4096


HIGHEST = lax.Precision.HIGHEST
EPSILON = 1e-06


def passed_along(block, axis, distance):
    devices = range(lax.axis_size(axis))
    route = [(i - distance, i) for i in devices if i - distance in devices]
    return lax.ppermute(block, axis, route)


def genome_begin(lengths, positions):
    ending = jnp.cumsum(lengths)
    starting = ending - lengths
    reached = starting[None, :] <= positions[:, None]
    return jnp.max(jnp.where(reached, starting[None, :], 0), axis=1)


def toeplitz(response):
    group_count, block = response.shape
    lag = jnp.arange(block, dtype=jnp.int32)
    picks = (lag[:, None, None] == lag[None, :, None] - lag[None, None, :]).astype(jnp.float32)
    return jnp.einsum("gk,kts->gts", response, picks, precision=HIGHEST)


def pole_tables(rate, angle, residue, block):
    counter = jnp.arange(block + 1).astype(jnp.float32)
    magnitude = jnp.exp(-rate[:, :, None] * counter)
    power_re = magnitude * jnp.cos(angle[:, :, None] * counter)
    power_im = magnitude * jnp.sin(angle[:, :, None] * counter)
    resid_re = residue[0][:, :, None]
    resid_im = residue[1][:, :, None]
    response = jnp.sum(
        resid_re * power_re[:, :, :block] - resid_im * power_im[:, :, :block], axis=1
    )
    enter_re = resid_re * power_re[:, :, 1:] - resid_im * power_im[:, :, 1:]
    enter_im = resid_re * power_im[:, :, 1:] + resid_im * power_re[:, :, 1:]
    entering = jnp.stack([enter_re, -enter_im])
    leaving = jnp.stack([power_re[:, :, block - 1 :: -1], power_im[:, :, block - 1 :: -1]])
    stepping = jnp.stack([power_re[:, :, block].T, power_im[:, :, block].T])
    return (toeplitz(response), entering, leaving, stepping)


def complex_times(factor_one, factor_two):
    return jnp.stack(
        [
            factor_one[0] * factor_two[0] - factor_one[1] * factor_two[1],
            factor_one[0] * factor_two[1] + factor_one[1] * factor_two[0],
        ]
    )


def block_terms(tables, columns, block_positions, block_starts):
    matrix_table, entering, leaving, stepping = tables
    same_genome = (block_positions[None, :] >= block_starts[:, None]).astype(jnp.float32)
    inside = jnp.einsum(
        "gts,gis->git", matrix_table * same_genome[None], columns, precision=HIGHEST
    )
    tail_mask = (block_positions >= block_starts[-1]).astype(jnp.float32)
    fresh_state = jnp.einsum("rgns,gis->rngi", leaving * tail_mask, columns, precision=HIGHEST)
    return (inside, fresh_state)


def carried(entering, carry_state):
    return jnp.einsum("rgnt,rngi->git", entering, carry_state, precision=HIGHEST)


def short_filter(padded, taps_part, positions, genome_start):
    lead = taps_part.shape[0] - 1
    row_count = positions.shape[0]
    result = jnp.zeros((row_count,) + padded.shape[1:], jnp.float32)
    for offset in range(taps_part.shape[0]):
        keep_tap = (positions - offset >= genome_start)[:, None, None]
        window = padded[lead - offset : lead - offset + row_count].astype(jnp.float32)
        result = result + jnp.where(keep_tap, taps_part[offset][None] * window, 0.0)
    return result


def on_device(qkv, taps, rate, angle, residue, skip, gain, lengths):
    tok_rows = qkv.shape[0]
    channels = qkv.shape[2]
    group_count = rate.shape[0]
    group_width = channels // group_count
    mode_count = rate.shape[1]
    reach = taps.shape[0]
    span_count = tok_rows // SPAN
    device = lax.axis_index("ctx")
    anchor = device * tok_rows
    positions = anchor + jnp.arange(tok_rows, dtype=jnp.int32)
    genome_start = genome_begin(lengths, positions)
    before = passed_along(qkv[tok_rows - (reach - 1) :], "ctx", 1)
    padded = jnp.concatenate([before, qkv], axis=0)
    filtered = short_filter(padded, taps, positions, genome_start)
    product = filtered[:, 1] * filtered[:, 2]
    tables = pole_tables(rate, angle, residue, SPAN)
    stepping = tables[3]
    values = jnp.transpose(
        product.reshape(span_count, SPAN, group_count, group_width), (0, 2, 3, 1)
    )
    span_pos = positions.reshape(span_count, SPAN)
    span_begin = genome_start.reshape(span_count, SPAN)
    summary = jnp.zeros((2, mode_count, group_count, group_width), jnp.float32)
    freshes = []
    keepers = []
    span_index = 0
    inside, fresh_state = block_terms(
        tables, values[span_index], span_pos[span_index], span_begin[span_index]
    )
    keep_state = span_begin[span_index, -1] < span_pos[span_index, 0]
    summary = jnp.where(keep_state, complex_times(stepping[..., None], summary), 0.0) + fresh_state
    insides = [inside]
    freshes.append(fresh_state)
    keepers.append(keep_state)
    device_count = lax.axis_size("ctx")
    reach = min(device_count, -(-(GENOME_MAX - 1) // tok_rows))
    starting = jnp.cumsum(lengths) - lengths

    def unbroken(first_row, last_row):
        hit = (starting >= first_row) & (starting <= last_row)
        return jnp.logical_not(jnp.any(hit))

    def widen(factor):
        return jnp.repeat(factor, group_width, axis=2)

    running = passed_along(summary.reshape(2, mode_count, channels), "ctx", 1)
    power = stepping
    distance = 1
    while distance < reach:
        earlier = passed_along(running, "ctx", distance)
        alive = unbroken(anchor - distance * tok_rows, anchor - 1)
        factor = widen(power) * alive.astype(jnp.float32)
        running = running + complex_times(factor, earlier)
        power = complex_times(power, power)
        distance = distance * 2
    incoming = running.reshape(2, mode_count, group_count, group_width)
    span_index = 0
    entered = (span_begin[span_index] < span_pos[span_index, 0])[None, None, :]
    outputs = [insides[span_index] + jnp.where(entered, carried(tables[1], incoming), 0.0)]
    stacked = jnp.stack(outputs, axis=0)
    long_part = jnp.transpose(stacked, (0, 3, 1, 2)).reshape(tok_rows, channels)
    gated_rows = filtered[:, 0] * (long_part + skip[None] * product)
    squares = lax.psum(jnp.sum(gated_rows * gated_rows, axis=1), "tp")
    root_mean = jnp.sqrt(squares / D + EPSILON)
    return (gated_rows / root_mean[:, None] * gain[None]).astype(jnp.bfloat16)


def solution(mesh):
    return jax.shard_map(
        on_device,
        mesh=mesh,
        in_specs=(
            P("ctx", None, "tp"),
            P(None, None, "tp"),
            P("tp", None),
            P("tp", None),
            P(None, "tp", None),
            P("tp"),
            P("tp"),
            P(),
        ),
        out_specs=P("ctx", "tp"),
        check_vma=False,
    )
```

```python
import jax
import jax.numpy as jnp
from jax import lax
from jax.sharding import PartitionSpec as P

D = 8192
SPAN = 128
GENOME_MAX = 4096


HIGHEST = lax.Precision.HIGHEST
EPSILON = 1e-06


def passed_along(block, axis, distance):
    devices = range(lax.axis_size(axis))
    route = [(i - distance, i) for i in devices if i - distance in devices]
    return lax.ppermute(block, axis, route)


def genome_begin(lengths, positions):
    ending = jnp.cumsum(lengths)
    starting = ending - lengths
    reached = starting[None, :] <= positions[:, None]
    return jnp.max(jnp.where(reached, starting[None, :], 0), axis=1)


def toeplitz(response):
    group_count, block = response.shape
    lag = jnp.arange(block, dtype=jnp.int32)
    picks = (lag[:, None, None] == lag[None, :, None] - lag[None, None, :]).astype(jnp.float32)
    return jnp.einsum("gk,kts->gts", response, picks, precision=HIGHEST)


def pole_tables(rate, angle, residue, block):
    counter = jnp.arange(block + 1).astype(jnp.float32)
    magnitude = jnp.exp(-rate[:, :, None] * counter)
    power_re = magnitude * jnp.cos(angle[:, :, None] * counter)
    power_im = magnitude * jnp.sin(angle[:, :, None] * counter)
    resid_re = residue[0][:, :, None]
    resid_im = residue[1][:, :, None]
    response = jnp.sum(
        resid_re * power_re[:, :, :block] - resid_im * power_im[:, :, :block], axis=1
    )
    enter_re = resid_re * power_re[:, :, 1:] - resid_im * power_im[:, :, 1:]
    enter_im = resid_re * power_im[:, :, 1:] + resid_im * power_re[:, :, 1:]
    entering = jnp.stack([enter_re, -enter_im])
    leaving = jnp.stack([power_re[:, :, block - 1 :: -1], power_im[:, :, block - 1 :: -1]])
    stepping = jnp.stack([power_re[:, :, block].T, power_im[:, :, block].T])
    return (toeplitz(response), entering, leaving, stepping)


def complex_times(factor_one, factor_two):
    return jnp.stack(
        [
            factor_one[0] * factor_two[0] - factor_one[1] * factor_two[1],
            factor_one[0] * factor_two[1] + factor_one[1] * factor_two[0],
        ]
    )


def block_terms(tables, columns, block_positions, block_starts):
    matrix_table, entering, leaving, stepping = tables
    same_genome = (block_positions[None, :] >= block_starts[:, None]).astype(jnp.float32)
    inside = jnp.einsum(
        "gts,gis->git", matrix_table * same_genome[None], columns, precision=HIGHEST
    )
    tail_mask = (block_positions >= block_starts[-1]).astype(jnp.float32)
    fresh_state = jnp.einsum("rgns,gis->rngi", leaving * tail_mask, columns, precision=HIGHEST)
    return (inside, fresh_state)


def carried(entering, carry_state):
    return jnp.einsum("rgnt,rngi->git", entering, carry_state, precision=HIGHEST)


def short_filter(padded, taps_part, positions, genome_start):
    lead = taps_part.shape[0] - 1
    row_count = positions.shape[0]
    result = jnp.zeros((row_count,) + padded.shape[1:], jnp.float32)
    for offset in range(taps_part.shape[0]):
        keep_tap = (positions - offset >= genome_start)[:, None, None]
        window = padded[lead - offset : lead - offset + row_count].astype(jnp.float32)
        result = result + jnp.where(keep_tap, taps_part[offset][None] * window, 0.0)
    return result


def on_device(qkv, taps, rate, angle, residue, skip, gain, lengths):
    tok_rows = qkv.shape[0]
    channels = qkv.shape[2]
    group_count = rate.shape[0]
    group_width = channels // group_count
    mode_count = rate.shape[1]
    reach = taps.shape[0]
    span_count = tok_rows // SPAN
    device = lax.axis_index("ctx")
    anchor = device * tok_rows
    positions = anchor + jnp.arange(tok_rows, dtype=jnp.int32)
    genome_start = genome_begin(lengths, positions)
    before = passed_along(qkv[tok_rows - (reach - 1) :], "ctx", 1)
    padded = jnp.concatenate([before, qkv], axis=0)
    filtered = short_filter(padded, taps, positions, genome_start)
    query, product = lax.optimization_barrier((filtered[:, 0], filtered[:, 1] * filtered[:, 2]))
    tables = pole_tables(rate, angle, residue, SPAN)
    stepping = tables[3]
    values = jnp.transpose(
        product.reshape(span_count, SPAN, group_count, group_width), (0, 2, 3, 1)
    )
    span_pos = positions.reshape(span_count, SPAN)
    span_begin = genome_start.reshape(span_count, SPAN)
    summary = jnp.zeros((2, mode_count, group_count, group_width), jnp.float32)
    freshes = []
    keepers = []
    span_index = 0
    inside, fresh_state = block_terms(
        tables, values[span_index], span_pos[span_index], span_begin[span_index]
    )
    keep_state = span_begin[span_index, -1] < span_pos[span_index, 0]
    summary = jnp.where(keep_state, complex_times(stepping[..., None], summary), 0.0) + fresh_state
    insides = [lax.optimization_barrier(inside)]
    freshes.append(fresh_state)
    keepers.append(keep_state)
    device_count = lax.axis_size("ctx")
    reach = min(device_count, -(-(GENOME_MAX - 1) // tok_rows))
    starting = jnp.cumsum(lengths) - lengths

    def unbroken(first_row, last_row):
        hit = (starting >= first_row) & (starting <= last_row)
        return jnp.logical_not(jnp.any(hit))

    def widen(factor):
        return jnp.repeat(factor, group_width, axis=2)

    running = passed_along(summary.reshape(2, mode_count, channels), "ctx", 1)
    power = stepping
    distance = 1
    while distance < reach:
        earlier = passed_along(running, "ctx", distance)
        alive = unbroken(anchor - distance * tok_rows, anchor - 1)
        factor = widen(power) * alive.astype(jnp.float32)
        running = running + complex_times(factor, earlier)
        power = complex_times(power, power)
        distance = distance * 2
    incoming = running.reshape(2, mode_count, group_count, group_width)
    span_index = 0
    entered = (span_begin[span_index] < span_pos[span_index, 0])[None, None, :]
    outputs = [insides[span_index] + jnp.where(entered, carried(tables[1], incoming), 0.0)]
    stacked = jnp.stack(outputs, axis=0)
    long_part = jnp.transpose(stacked, (0, 3, 1, 2)).reshape(tok_rows, channels)
    gated_rows = query * (long_part + skip[None] * product)
    partial = jnp.sum(gated_rows * gated_rows, axis=1)
    squares = jnp.sum(lax.all_gather(partial, "tp", axis=0), axis=0)
    root_mean = jnp.sqrt(squares / D + EPSILON)
    return (gated_rows / root_mean[:, None] * gain[None]).astype(jnp.bfloat16)


def solution(mesh):
    return jax.shard_map(
        on_device,
        mesh=mesh,
        in_specs=(
            P("ctx", None, "tp"),
            P(None, None, "tp"),
            P("tp", None),
            P("tp", None),
            P(None, "tp", None),
            P("tp"),
            P("tp"),
            P(),
        ),
        out_specs=P("ctx", "tp"),
        check_vma=False,
    )
```

```python
import jax
import jax.numpy as jnp
from jax import lax
from jax.sharding import PartitionSpec as P

D = 8192
SPAN = 128
GENOME_MAX = 4096


HIGHEST = lax.Precision.HIGHEST
EPSILON = 1e-06


def passed_along(block, axis, distance):
    devices = range(lax.axis_size(axis))
    route = [(i - distance, i) for i in devices if i - distance in devices]
    return lax.ppermute(block, axis, route)


def genome_begin(lengths, positions):
    ending = jnp.cumsum(lengths)
    starting = ending - lengths
    reached = starting[None, :] <= positions[:, None]
    return jnp.max(jnp.where(reached, starting[None, :], 0), axis=1)


def toeplitz(response):
    group_count, block = response.shape
    lag = jnp.arange(block, dtype=jnp.int32)
    picks = (lag[:, None, None] == lag[None, :, None] - lag[None, None, :]).astype(jnp.float32)
    return jnp.einsum("gk,kts->gts", response, picks, precision=HIGHEST)


def pole_tables(rate, angle, residue, block):
    counter = jnp.arange(block + 1).astype(jnp.float32)
    magnitude = jnp.exp(-rate[:, :, None] * counter)
    power_re = magnitude * jnp.cos(angle[:, :, None] * counter)
    power_im = magnitude * jnp.sin(angle[:, :, None] * counter)
    resid_re = residue[0][:, :, None]
    resid_im = residue[1][:, :, None]
    response = jnp.sum(
        resid_re * power_re[:, :, :block] - resid_im * power_im[:, :, :block], axis=1
    )
    enter_re = resid_re * power_re[:, :, 1:] - resid_im * power_im[:, :, 1:]
    enter_im = resid_re * power_im[:, :, 1:] + resid_im * power_re[:, :, 1:]
    entering = jnp.stack([enter_re, -enter_im])
    leaving = jnp.stack([power_re[:, :, block - 1 :: -1], power_im[:, :, block - 1 :: -1]])
    stepping = jnp.stack([power_re[:, :, block].T, power_im[:, :, block].T])
    return (toeplitz(response), entering, leaving, stepping)


def complex_times(factor_one, factor_two):
    return jnp.stack(
        [
            factor_one[0] * factor_two[0] - factor_one[1] * factor_two[1],
            factor_one[0] * factor_two[1] + factor_one[1] * factor_two[0],
        ]
    )


def block_terms(tables, columns, block_positions, block_starts):
    matrix_table, entering, leaving, stepping = tables
    same_genome = (block_positions[None, :] >= block_starts[:, None]).astype(jnp.float32)
    inside = jnp.einsum(
        "gts,gis->git", matrix_table * same_genome[None], columns, precision=HIGHEST
    )
    tail_mask = (block_positions >= block_starts[-1]).astype(jnp.float32)
    fresh_state = jnp.einsum("rgns,gis->rngi", leaving * tail_mask, columns, precision=HIGHEST)
    return (inside, fresh_state)


def carried(entering, carry_state):
    return jnp.einsum("rgnt,rngi->git", entering, carry_state, precision=HIGHEST)


def short_filter(padded, taps_part, positions, genome_start):
    lead = taps_part.shape[0] - 1
    row_count = positions.shape[0]
    result = jnp.zeros((row_count,) + padded.shape[1:], jnp.float32)
    for offset in range(taps_part.shape[0]):
        keep_tap = (positions - offset >= genome_start)[:, None, None]
        window = padded[lead - offset : lead - offset + row_count].astype(jnp.float32)
        result = result + jnp.where(keep_tap, taps_part[offset][None] * window, 0.0)
    return result


def on_device(qkv, taps, rate, angle, residue, skip, gain, lengths):
    tok_rows = qkv.shape[0]
    channels = qkv.shape[2]
    group_count = rate.shape[0]
    group_width = channels // group_count
    mode_count = rate.shape[1]
    reach = taps.shape[0]
    span_count = tok_rows // SPAN
    device = lax.axis_index("ctx")
    anchor = device * tok_rows
    positions = anchor + jnp.arange(tok_rows, dtype=jnp.int32)
    genome_start = genome_begin(lengths, positions)
    before = passed_along(qkv[tok_rows - (reach - 1) :], "ctx", 1)
    padded = jnp.concatenate([before, qkv], axis=0)
    filtered = short_filter(padded, taps, positions, genome_start)
    query, product = lax.optimization_barrier((filtered[:, 0], filtered[:, 1] * filtered[:, 2]))
    tables = pole_tables(rate, angle, residue, SPAN)
    stepping = tables[3]
    values = jnp.transpose(
        product.reshape(span_count, SPAN, group_count, group_width), (0, 2, 3, 1)
    )
    span_pos = positions.reshape(span_count, SPAN)
    span_begin = genome_start.reshape(span_count, SPAN)
    summary = jnp.zeros((2, mode_count, group_count, group_width), jnp.float32)
    freshes = []
    keepers = []
    span_index = 0
    inside, fresh_state = block_terms(
        tables, values[span_index], span_pos[span_index], span_begin[span_index]
    )
    keep_state = span_begin[span_index, -1] < span_pos[span_index, 0]
    summary = jnp.where(keep_state, complex_times(stepping[..., None], summary), 0.0) + fresh_state
    insides = [lax.optimization_barrier(inside)]
    freshes.append(fresh_state)
    keepers.append(keep_state)
    device_count = lax.axis_size("ctx")
    reach = min(device_count, -(-(GENOME_MAX - 1) // tok_rows))
    starting = jnp.cumsum(lengths) - lengths

    def unbroken(first_row, last_row):
        hit = (starting >= first_row) & (starting <= last_row)
        return jnp.logical_not(jnp.any(hit))

    def widen(factor):
        return jnp.repeat(factor, group_width, axis=2)

    running = passed_along(summary.reshape(2, mode_count, channels), "ctx", 1)
    power = stepping
    distance = 1
    while distance < reach:
        earlier = passed_along(running, "ctx", distance)
        alive = unbroken(anchor - distance * tok_rows, anchor - 1)
        factor = widen(power) * alive.astype(jnp.float32)
        running = running + complex_times(factor, earlier)
        power = complex_times(power, power)
        distance = distance * 2
    incoming = running.reshape(2, mode_count, group_count, group_width)
    span_index = 0
    entered = (span_begin[span_index] < span_pos[span_index, 0])[None, None, :]
    outputs = [insides[span_index] + jnp.where(entered, carried(tables[1], incoming), 0.0)]
    stacked = jnp.stack(outputs, axis=0)
    long_part = jnp.transpose(stacked, (0, 3, 1, 2)).reshape(tok_rows, channels)
    gated_rows = query * (long_part + skip[None] * product)
    partial = jnp.sum(gated_rows * gated_rows, axis=1)
    squares = partial
    span = 1
    while span < lax.axis_size("tp"):
        pairs = [(i, i ^ span) for i in range(lax.axis_size("tp"))]
        squares = squares + lax.ppermute(squares, "tp", pairs)
        span = span * 2
    root_mean = jnp.sqrt(squares / D + EPSILON)
    return (gated_rows / root_mean[:, None] * gain[None]).astype(jnp.bfloat16)


def solution(mesh):
    return jax.shard_map(
        on_device,
        mesh=mesh,
        in_specs=(
            P("ctx", None, "tp"),
            P(None, None, "tp"),
            P("tp", None),
            P("tp", None),
            P(None, "tp", None),
            P("tp"),
            P("tp"),
            P(),
        ),
        out_specs=P("ctx", "tp"),
        check_vma=False,
    )
```

```python
import jax
import jax.numpy as jnp
from jax import lax
from jax.sharding import PartitionSpec as P

D = 8192
SPAN = 128
GENOME_MAX = 4096


HIGHEST = lax.Precision.HIGHEST
HIGH = lax.Precision.HIGH
EPSILON = 1e-06


def passed_along(block, axis, distance):
    devices = range(lax.axis_size(axis))
    route = [(i - distance, i) for i in devices if i - distance in devices]
    return lax.ppermute(block, axis, route)


def genome_begin(lengths, positions):
    ending = jnp.cumsum(lengths)
    starting = ending - lengths
    reached = starting[None, :] <= positions[:, None]
    return jnp.max(jnp.where(reached, starting[None, :], 0), axis=1)


def toeplitz(response):
    group_count, block = response.shape
    lag = jnp.arange(block, dtype=jnp.int32)
    picks = (lag[:, None, None] == lag[None, :, None] - lag[None, None, :]).astype(jnp.float32)
    return jnp.einsum("gk,kts->gts", response, picks, precision=HIGHEST)


def pole_tables(rate, angle, residue, block):
    counter = jnp.arange(block + 1).astype(jnp.float32)
    magnitude = jnp.exp(-rate[:, :, None] * counter)
    power_re = magnitude * jnp.cos(angle[:, :, None] * counter)
    power_im = magnitude * jnp.sin(angle[:, :, None] * counter)
    resid_re = residue[0][:, :, None]
    resid_im = residue[1][:, :, None]
    response = jnp.sum(
        resid_re * power_re[:, :, :block] - resid_im * power_im[:, :, :block], axis=1
    )
    enter_re = resid_re * power_re[:, :, 1:] - resid_im * power_im[:, :, 1:]
    enter_im = resid_re * power_im[:, :, 1:] + resid_im * power_re[:, :, 1:]
    entering = jnp.stack([enter_re, -enter_im])
    leaving = jnp.stack([power_re[:, :, block - 1 :: -1], power_im[:, :, block - 1 :: -1]])
    stepping = jnp.stack([power_re[:, :, block].T, power_im[:, :, block].T])
    return (response, entering, leaving, stepping)


def complex_times(factor_one, factor_two):
    return jnp.stack(
        [
            factor_one[0] * factor_two[0] - factor_one[1] * factor_two[1],
            factor_one[0] * factor_two[1] + factor_one[1] * factor_two[0],
        ]
    )


def inside_terms(matrix_table, columns, block_positions, block_starts):
    same_genome = (block_positions[None, :] >= block_starts[:, None]).astype(jnp.float32)
    return jnp.einsum("gts,gis->git", matrix_table * same_genome[None], columns, precision=HIGH)


def fresh_terms(leaving, columns, block_positions, block_starts):
    tail_mask = (block_positions >= block_starts[-1]).astype(jnp.float32)
    return jnp.einsum("rgns,gis->rngi", leaving * tail_mask, columns, precision=HIGH)


def carried(entering, carry_state):
    return jnp.einsum("rgnt,rngi->git", entering, carry_state, precision=HIGH)


def short_filter(padded, taps_part, positions, genome_start):
    lead = taps_part.shape[0] - 1
    row_count = positions.shape[0]
    result = jnp.zeros((row_count,) + padded.shape[1:], jnp.float32)
    for offset in range(taps_part.shape[0]):
        keep_tap = (positions - offset >= genome_start)[:, None, None]
        window = padded[lead - offset : lead - offset + row_count].astype(jnp.float32)
        result = result + jnp.where(keep_tap, taps_part[offset][None] * window, 0.0)
    return result


def on_device(qkv, taps, rate, angle, residue, skip, gain, lengths):
    tok_rows = qkv.shape[0]
    channels = qkv.shape[2]
    group_count = rate.shape[0]
    group_width = channels // group_count
    mode_count = rate.shape[1]
    reach = taps.shape[0]
    span_count = tok_rows // SPAN
    device = lax.axis_index("ctx")
    anchor = device * tok_rows
    positions = anchor + jnp.arange(tok_rows, dtype=jnp.int32)
    genome_start = genome_begin(lengths, positions)
    before = passed_along(qkv[tok_rows - (reach - 1) :], "ctx", 1)
    padded = jnp.concatenate([before, qkv], axis=0)
    filtered = short_filter(padded, taps, positions, genome_start)
    query, product = lax.optimization_barrier((filtered[:, 0], filtered[:, 1] * filtered[:, 2]))
    tables = pole_tables(rate, angle, residue, SPAN)
    stepping = tables[3]
    values = jnp.transpose(
        product.reshape(span_count, SPAN, group_count, group_width), (0, 2, 3, 1)
    )
    span_pos = positions.reshape(span_count, SPAN)
    span_begin = genome_start.reshape(span_count, SPAN)
    summary = jnp.zeros((2, mode_count, group_count, group_width), jnp.float32)
    freshes = []
    keepers = []
    span_index = 0
    fresh_state = fresh_terms(
        tables[2], values[span_index], span_pos[span_index], span_begin[span_index]
    )
    keep_state = span_begin[span_index, -1] < span_pos[span_index, 0]
    summary = jnp.where(keep_state, complex_times(stepping[..., None], summary), 0.0) + fresh_state
    freshes.append(fresh_state)
    keepers.append(keep_state)
    device_count = lax.axis_size("ctx")
    reach = min(device_count, -(-(GENOME_MAX - 1) // tok_rows))
    starting = jnp.cumsum(lengths) - lengths

    def unbroken(first_row, last_row):
        hit = (starting >= first_row) & (starting <= last_row)
        return jnp.logical_not(jnp.any(hit))

    def widen(factor):
        return jnp.repeat(factor, group_width, axis=2)

    running = passed_along(summary.reshape(2, mode_count, channels), "ctx", 1)
    response, running = lax.optimization_barrier((tables[0], running))
    inside = inside_terms(
        toeplitz(response), values[span_index], span_pos[span_index], span_begin[span_index]
    )
    insides = [lax.optimization_barrier(inside)]
    power = stepping
    distance = 1
    while distance < reach:
        earlier = passed_along(running, "ctx", distance)
        alive = unbroken(anchor - distance * tok_rows, anchor - 1)
        factor = widen(power) * alive.astype(jnp.float32)
        running = running + complex_times(factor, earlier)
        power = complex_times(power, power)
        distance = distance * 2
    incoming = running.reshape(2, mode_count, group_count, group_width)
    span_index = 0
    entered = (span_begin[span_index] < span_pos[span_index, 0])[None, None, :]
    outputs = [insides[span_index] + jnp.where(entered, carried(tables[1], incoming), 0.0)]
    stacked = jnp.stack(outputs, axis=0)
    long_part = jnp.transpose(stacked, (0, 3, 1, 2)).reshape(tok_rows, channels)
    gated_rows = query * (long_part + skip[None] * product)
    partial = jnp.sum(gated_rows * gated_rows, axis=1)
    squares = partial
    span = 1
    while span < lax.axis_size("tp"):
        pairs = [(i, i ^ span) for i in range(lax.axis_size("tp"))]
        squares = squares + lax.ppermute(squares, "tp", pairs)
        span = span * 2
    root_mean = jnp.sqrt(squares / D + EPSILON)
    return (gated_rows / root_mean[:, None] * gain[None]).astype(jnp.bfloat16)


def solution(mesh):
    return jax.shard_map(
        on_device,
        mesh=mesh,
        in_specs=(
            P("ctx", None, "tp"),
            P(None, None, "tp"),
            P("tp", None),
            P("tp", None),
            P(None, "tp", None),
            P("tp"),
            P("tp"),
            P(),
        ),
        out_specs=P("ctx", "tp"),
        check_vma=False,
    )
```

```python
import jax
import jax.numpy as jnp
from jax import lax
from jax.sharding import PartitionSpec as P

D = 8192
SPAN = 128
GENOME_MAX = 4096


HIGHEST = lax.Precision.HIGHEST
HIGH = lax.Precision.HIGH
EPSILON = 1e-06


def passed_along(block, axis, distance):
    devices = range(lax.axis_size(axis))
    route = [(i - distance, i) for i in devices if i - distance in devices]
    return lax.ppermute(block, axis, route)


def genome_begin(lengths, positions):
    ending = jnp.cumsum(lengths)
    starting = ending - lengths
    reached = starting[None, :] <= positions[:, None]
    return jnp.max(jnp.where(reached, starting[None, :], 0), axis=1)


def toeplitz(response):
    group_count, block = response.shape
    lag = jnp.arange(block, dtype=jnp.int32)
    picks = (lag[:, None, None] == lag[None, :, None] - lag[None, None, :]).astype(jnp.float32)
    return jnp.einsum("gk,kts->gts", response, picks, precision=HIGHEST)


def pole_tables(rate, angle, residue, block):
    counter = jnp.arange(block + 1).astype(jnp.float32)
    magnitude = jnp.exp(-rate[:, :, None] * counter)
    power_re = magnitude * jnp.cos(angle[:, :, None] * counter)
    power_im = magnitude * jnp.sin(angle[:, :, None] * counter)
    resid_re = residue[0][:, :, None]
    resid_im = residue[1][:, :, None]
    response = jnp.sum(
        resid_re * power_re[:, :, :block] - resid_im * power_im[:, :, :block], axis=1
    )
    enter_re = resid_re * power_re[:, :, 1:] - resid_im * power_im[:, :, 1:]
    enter_im = resid_re * power_im[:, :, 1:] + resid_im * power_re[:, :, 1:]
    entering = jnp.stack([enter_re, -enter_im])
    leaving = jnp.stack([power_re[:, :, block - 1 :: -1], power_im[:, :, block - 1 :: -1]])
    stepping = jnp.stack([power_re[:, :, block].T, power_im[:, :, block].T])
    return (response, entering, leaving, stepping)


def pole_exits(rate, angle, block):
    counter = (block - 1 - jnp.arange(block)).astype(jnp.float32)
    magnitude = jnp.exp(-rate[:, :, None] * counter)
    leaving = jnp.stack(
        [magnitude * jnp.cos(angle[:, :, None] * counter), magnitude * jnp.sin(angle[:, :, None] * counter)]
    )
    last = jnp.float32(block)
    step_size = jnp.exp(-rate * last)
    stepping = jnp.stack([(step_size * jnp.cos(angle * last)).T, (step_size * jnp.sin(angle * last)).T])
    return (leaving, stepping)


def complex_times(factor_one, factor_two):
    return jnp.stack(
        [
            factor_one[0] * factor_two[0] - factor_one[1] * factor_two[1],
            factor_one[0] * factor_two[1] + factor_one[1] * factor_two[0],
        ]
    )


def inside_terms(matrix_table, columns, block_positions, block_starts):
    same_genome = (block_positions[None, :] >= block_starts[:, None]).astype(jnp.float32)
    return jnp.einsum("gts,gis->git", matrix_table * same_genome[None], columns, precision=HIGH)


def fresh_terms(leaving, columns, block_positions, block_starts):
    tail_mask = (block_positions >= block_starts[-1]).astype(jnp.float32)
    return jnp.einsum("rgns,gis->rngi", leaving * tail_mask, columns, precision=HIGH)


def carried(entering, carry_state):
    return jnp.einsum("rgnt,rngi->git", entering, carry_state, precision=HIGH)


def short_filter(padded, taps_part, positions, genome_start):
    lead = taps_part.shape[0] - 1
    row_count = positions.shape[0]
    result = jnp.zeros((row_count,) + padded.shape[1:], jnp.float32)
    for offset in range(taps_part.shape[0]):
        keep_tap = (positions - offset >= genome_start)[:, None, None]
        window = padded[lead - offset : lead - offset + row_count].astype(jnp.float32)
        result = result + jnp.where(keep_tap, taps_part[offset][None] * window, 0.0)
    return result


def on_device(qkv, taps, rate, angle, residue, skip, gain, lengths):
    tok_rows = qkv.shape[0]
    channels = qkv.shape[2]
    group_count = rate.shape[0]
    group_width = channels // group_count
    mode_count = rate.shape[1]
    reach = taps.shape[0]
    span_count = tok_rows // SPAN
    device = lax.axis_index("ctx")
    anchor = device * tok_rows
    positions = anchor + jnp.arange(tok_rows, dtype=jnp.int32)
    genome_start = genome_begin(lengths, positions)
    before = passed_along(qkv[tok_rows - (reach - 1) :], "ctx", 1)
    padded = jnp.concatenate([before, qkv], axis=0)
    filtered = short_filter(padded, taps, positions, genome_start)
    query, product = lax.optimization_barrier((filtered[:, 0], filtered[:, 1] * filtered[:, 2]))
    leaving, stepping = pole_exits(rate, angle, SPAN)
    values = jnp.transpose(
        product.reshape(span_count, SPAN, group_count, group_width), (0, 2, 3, 1)
    )
    span_pos = positions.reshape(span_count, SPAN)
    span_begin = genome_start.reshape(span_count, SPAN)
    summary = jnp.zeros((2, mode_count, group_count, group_width), jnp.float32)
    freshes = []
    keepers = []
    span_index = 0
    fresh_state = fresh_terms(
        leaving, values[span_index], span_pos[span_index], span_begin[span_index]
    )
    keep_state = span_begin[span_index, -1] < span_pos[span_index, 0]
    summary = jnp.where(keep_state, complex_times(stepping[..., None], summary), 0.0) + fresh_state
    freshes.append(fresh_state)
    keepers.append(keep_state)
    device_count = lax.axis_size("ctx")
    reach = min(device_count, -(-(GENOME_MAX - 1) // tok_rows))
    starting = jnp.cumsum(lengths) - lengths

    def unbroken(first_row, last_row):
        hit = (starting >= first_row) & (starting <= last_row)
        return jnp.logical_not(jnp.any(hit))

    def widen(factor):
        return jnp.repeat(factor, group_width, axis=2)

    running = passed_along(summary.reshape(2, mode_count, channels), "ctx", 1)
    pole_inputs, running = lax.optimization_barrier(((rate, angle, residue), running))
    tables = pole_tables(*pole_inputs, SPAN)
    response = tables[0]
    inside = inside_terms(
        toeplitz(response), values[span_index], span_pos[span_index], span_begin[span_index]
    )
    insides = [lax.optimization_barrier(inside)]
    power = stepping
    distance = 1
    while distance < reach:
        earlier = passed_along(running, "ctx", distance)
        alive = unbroken(anchor - distance * tok_rows, anchor - 1)
        factor = widen(power) * alive.astype(jnp.float32)
        running = running + complex_times(factor, earlier)
        power = complex_times(power, power)
        distance = distance * 2
    incoming = running.reshape(2, mode_count, group_count, group_width)
    span_index = 0
    entered = (span_begin[span_index] < span_pos[span_index, 0])[None, None, :]
    outputs = [insides[span_index] + jnp.where(entered, carried(tables[1], incoming), 0.0)]
    stacked = jnp.stack(outputs, axis=0)
    long_part = jnp.transpose(stacked, (0, 3, 1, 2)).reshape(tok_rows, channels)
    gated_rows = query * (long_part + skip[None] * product)
    partial = jnp.sum(gated_rows * gated_rows, axis=1)
    squares = partial
    span = 1
    while span < lax.axis_size("tp"):
        pairs = [(i, i ^ span) for i in range(lax.axis_size("tp"))]
        squares = squares + lax.ppermute(squares, "tp", pairs)
        span = span * 2
    root_mean = jnp.sqrt(squares / D + EPSILON)
    return (gated_rows / root_mean[:, None] * gain[None]).astype(jnp.bfloat16)


def solution(mesh):
    return jax.shard_map(
        on_device,
        mesh=mesh,
        in_specs=(
            P("ctx", None, "tp"),
            P(None, None, "tp"),
            P("tp", None),
            P("tp", None),
            P(None, "tp", None),
            P("tp"),
            P("tp"),
            P(),
        ),
        out_specs=P("ctx", "tp"),
        check_vma=False,
    )
```

```python
import jax
import jax.numpy as jnp
from jax import lax
from jax.sharding import PartitionSpec as P

D = 8192
SPAN = 128
GENOME_MAX = 4096


HIGHEST = lax.Precision.HIGHEST
HIGH = lax.Precision.HIGH
EPSILON = 1e-06


def passed_along(block, axis, distance):
    devices = range(lax.axis_size(axis))
    route = [(i - distance, i) for i in devices if i - distance in devices]
    return lax.ppermute(block, axis, route)


def genome_begin(lengths, positions):
    ending = jnp.cumsum(lengths)
    starting = ending - lengths
    reached = starting[None, :] <= positions[:, None]
    return jnp.max(jnp.where(reached, starting[None, :], 0), axis=1)


def toeplitz(response):
    group_count, block = response.shape
    lag = jnp.arange(block, dtype=jnp.int32)
    picks = (lag[:, None, None] == lag[None, :, None] - lag[None, None, :]).astype(jnp.float32)
    return jnp.einsum("gk,kts->gts", response, picks, precision=HIGHEST)


def pole_tables(rate, angle, residue, block):
    counter = jnp.arange(block + 1).astype(jnp.float32)
    magnitude = jnp.exp(-rate[:, :, None] * counter)
    power_re = magnitude * jnp.cos(angle[:, :, None] * counter)
    power_im = magnitude * jnp.sin(angle[:, :, None] * counter)
    resid_re = residue[0][:, :, None]
    resid_im = residue[1][:, :, None]
    response = jnp.sum(
        resid_re * power_re[:, :, :block] - resid_im * power_im[:, :, :block], axis=1
    )
    enter_re = resid_re * power_re[:, :, 1:] - resid_im * power_im[:, :, 1:]
    enter_im = resid_re * power_im[:, :, 1:] + resid_im * power_re[:, :, 1:]
    entering = jnp.stack([enter_re, -enter_im])
    leaving = jnp.stack([power_re[:, :, block - 1 :: -1], power_im[:, :, block - 1 :: -1]])
    stepping = jnp.stack([power_re[:, :, block].T, power_im[:, :, block].T])
    return (response, entering, leaving, stepping)


def pole_exits(rate, angle, block):
    counter = (block - 1 - jnp.arange(block)).astype(jnp.float32)
    magnitude = jnp.exp(-rate[:, :, None] * counter)
    leaving = jnp.stack(
        [magnitude * jnp.cos(angle[:, :, None] * counter), magnitude * jnp.sin(angle[:, :, None] * counter)]
    )
    last = jnp.float32(block)
    step_size = jnp.exp(-rate * last)
    stepping = jnp.stack([(step_size * jnp.cos(angle * last)).T, (step_size * jnp.sin(angle * last)).T])
    return (leaving, stepping)


def complex_times(factor_one, factor_two):
    return jnp.stack(
        [
            factor_one[0] * factor_two[0] - factor_one[1] * factor_two[1],
            factor_one[0] * factor_two[1] + factor_one[1] * factor_two[0],
        ]
    )


def inside_terms(matrix_table, columns, block_positions, block_starts):
    same_genome = (block_positions[None, :] >= block_starts[:, None]).astype(jnp.float32)
    return jnp.einsum("gts,gis->git", matrix_table * same_genome[None], columns, precision=HIGH)


def fresh_terms(leaving, columns, block_positions, block_starts):
    tail_mask = (block_positions >= block_starts[-1]).astype(jnp.float32)
    return jnp.einsum("rgns,gis->rngi", leaving * tail_mask, columns, precision=HIGH)


def carried(entering, carry_state):
    return jnp.einsum("rgnt,rngi->git", entering, carry_state, precision=HIGH)


def short_filter(padded, taps_part, positions, genome_start):
    lead = taps_part.shape[0] - 1
    row_count = positions.shape[0]
    result = jnp.zeros((row_count,) + padded.shape[1:], jnp.float32)
    for offset in range(taps_part.shape[0]):
        keep_tap = (positions - offset >= genome_start)[:, None, None]
        window = padded[lead - offset : lead - offset + row_count].astype(jnp.float32)
        result = result + jnp.where(keep_tap, taps_part[offset][None] * window, 0.0)
    return result


def on_device(qkv, taps, rate, angle, residue, skip, gain, lengths):
    tok_rows = qkv.shape[0]
    channels = qkv.shape[2]
    group_count = rate.shape[0]
    group_width = channels // group_count
    mode_count = rate.shape[1]
    reach = taps.shape[0]
    span_count = tok_rows // SPAN
    device = lax.axis_index("ctx")
    anchor = device * tok_rows
    positions = anchor + jnp.arange(tok_rows, dtype=jnp.int32)
    genome_start = genome_begin(lengths, positions)
    before = passed_along(qkv[tok_rows - (reach - 1) :], "ctx", 1)
    padded = jnp.concatenate([before, qkv], axis=0)
    filtered = short_filter(padded, taps, positions, genome_start)
    query, product = lax.optimization_barrier((filtered[:, 0], filtered[:, 1] * filtered[:, 2]))
    leaving, stepping = pole_exits(rate, angle, SPAN)
    values = jnp.transpose(
        product.reshape(span_count, SPAN, group_count, group_width), (0, 2, 3, 1)
    )
    span_pos = positions.reshape(span_count, SPAN)
    span_begin = genome_start.reshape(span_count, SPAN)
    summary = jnp.zeros((2, mode_count, group_count, group_width), jnp.float32)
    freshes = []
    keepers = []
    span_index = 0
    fresh_state = fresh_terms(
        leaving, values[span_index], span_pos[span_index], span_begin[span_index]
    )
    keep_state = span_begin[span_index, -1] < span_pos[span_index, 0]
    summary = jnp.where(keep_state, complex_times(stepping[..., None], summary), 0.0) + fresh_state
    freshes.append(fresh_state)
    keepers.append(keep_state)
    device_count = lax.axis_size("ctx")
    reach = min(device_count, -(-(GENOME_MAX - 1) // tok_rows))
    starting = jnp.cumsum(lengths) - lengths

    def unbroken(first_row, last_row):
        hit = (starting >= first_row) & (starting <= last_row)
        return jnp.logical_not(jnp.any(hit))

    def widen(factor):
        return jnp.repeat(factor, group_width, axis=2)

    running = passed_along(summary.reshape(2, mode_count, channels), "ctx", 1)
    pole_inputs, running = lax.optimization_barrier(((rate, angle, residue), running))
    tables = pole_tables(*pole_inputs, SPAN)
    response = tables[0]
    inside = inside_terms(
        toeplitz(response), values[span_index], span_pos[span_index], span_begin[span_index]
    )
    insides = [lax.optimization_barrier(inside)]
    distances = []
    ladder = [stepping]
    while 2 ** len(distances) < reach:
        distances.append(2 ** len(distances))
        ladder.append(complex_times(ladder[-1], ladder[-1]))
    alive = jnp.stack([unbroken(anchor - step * tok_rows, anchor - 1) for step in distances])
    factors = jnp.repeat(jnp.stack(ladder[: len(distances)]), group_width, axis=3)
    factors = factors * alive.astype(jnp.float32)[:, None, None, None]
    for index, distance in enumerate(distances):
        earlier = passed_along(running, "ctx", distance)
        running = running + complex_times(factors[index], earlier)
    incoming = running.reshape(2, mode_count, group_count, group_width)
    span_index = 0
    entered = (span_begin[span_index] < span_pos[span_index, 0])[None, None, :]
    outputs = [insides[span_index] + jnp.where(entered, carried(tables[1], incoming), 0.0)]
    stacked = jnp.stack(outputs, axis=0)
    long_part = jnp.transpose(stacked, (0, 3, 1, 2)).reshape(tok_rows, channels)
    gated_rows = query * (long_part + skip[None] * product)
    partial = jnp.sum(gated_rows * gated_rows, axis=1)
    squares = partial
    span = 1
    while span < lax.axis_size("tp"):
        pairs = [(i, i ^ span) for i in range(lax.axis_size("tp"))]
        squares = squares + lax.ppermute(squares, "tp", pairs)
        span = span * 2
    root_mean = jnp.sqrt(squares / D + EPSILON)
    return (gated_rows / root_mean[:, None] * gain[None]).astype(jnp.bfloat16)


def solution(mesh):
    return jax.shard_map(
        on_device,
        mesh=mesh,
        in_specs=(
            P("ctx", None, "tp"),
            P(None, None, "tp"),
            P("tp", None),
            P("tp", None),
            P(None, "tp", None),
            P("tp"),
            P("tp"),
            P(),
        ),
        out_specs=P("ctx", "tp"),
        check_vma=False,
    )
```

```python
import jax
import jax.numpy as jnp
from jax import lax
from jax.sharding import PartitionSpec as P

D = 8192
SPAN = 128
GENOME_MAX = 4096


HIGHEST = lax.Precision.HIGHEST
HIGH = lax.Precision.HIGH
EPSILON = 1e-06


def passed_along(block, axis, distance):
    devices = range(lax.axis_size(axis))
    route = [(i - distance, i) for i in devices if i - distance in devices]
    return lax.ppermute(block, axis, route)


def genome_begin(lengths, positions):
    ending = jnp.cumsum(lengths)
    starting = ending - lengths
    reached = starting[None, :] <= positions[:, None]
    return jnp.max(jnp.where(reached, starting[None, :], 0), axis=1)


def toeplitz(response):
    group_count, block = response.shape
    lag = jnp.arange(block, dtype=jnp.int32)
    picks = (lag[:, None, None] == lag[None, :, None] - lag[None, None, :]).astype(jnp.float32)
    return jnp.einsum("gk,kts->gts", response, picks, precision=HIGHEST)


def pole_tables(rate, angle, residue, block):
    counter = jnp.arange(block + 1).astype(jnp.float32)
    magnitude = jnp.exp(-rate[:, :, None] * counter)
    power_re = magnitude * jnp.cos(angle[:, :, None] * counter)
    power_im = magnitude * jnp.sin(angle[:, :, None] * counter)
    resid_re = residue[0][:, :, None]
    resid_im = residue[1][:, :, None]
    response = jnp.sum(
        resid_re * power_re[:, :, :block] - resid_im * power_im[:, :, :block], axis=1
    )
    enter_re = resid_re * power_re[:, :, 1:] - resid_im * power_im[:, :, 1:]
    enter_im = resid_re * power_im[:, :, 1:] + resid_im * power_re[:, :, 1:]
    entering = jnp.stack([enter_re, -enter_im])
    leaving = jnp.stack([power_re[:, :, block - 1 :: -1], power_im[:, :, block - 1 :: -1]])
    stepping = jnp.stack([power_re[:, :, block].T, power_im[:, :, block].T])
    return (response, entering, leaving, stepping)


def pole_exits(rate, angle, block):
    counter = (block - 1 - jnp.arange(block)).astype(jnp.float32)
    magnitude = jnp.exp(-rate[:, :, None] * counter)
    leaving = jnp.stack(
        [magnitude * jnp.cos(angle[:, :, None] * counter), magnitude * jnp.sin(angle[:, :, None] * counter)]
    )
    last = jnp.float32(block)
    step_size = jnp.exp(-rate * last)
    stepping = jnp.stack([(step_size * jnp.cos(angle * last)).T, (step_size * jnp.sin(angle * last)).T])
    return (leaving, stepping)


def complex_times(factor_one, factor_two):
    return jnp.stack(
        [
            factor_one[0] * factor_two[0] - factor_one[1] * factor_two[1],
            factor_one[0] * factor_two[1] + factor_one[1] * factor_two[0],
        ]
    )


def inside_terms(matrix_table, columns, block_positions, block_starts):
    same_genome = (block_positions[None, :] >= block_starts[:, None]).astype(jnp.float32)
    return jnp.einsum("gts,gis->git", matrix_table * same_genome[None], columns, precision=HIGH)


def fresh_terms(leaving, columns, block_positions, block_starts):
    tail_mask = (block_positions >= block_starts[-1]).astype(jnp.float32)
    return jnp.einsum("rgns,gis->rngi", leaving * tail_mask, columns, precision=HIGH)


def carried(entering, carry_state):
    return jnp.einsum("rgnt,rngi->git", entering, carry_state, precision=HIGH)


def short_filter(padded, taps_part, positions, genome_start):
    lead = taps_part.shape[0] - 1
    row_count = positions.shape[0]
    result = jnp.zeros((row_count,) + padded.shape[1:], jnp.float32)
    for offset in range(taps_part.shape[0]):
        keep_tap = (positions - offset >= genome_start)[:, None, None]
        window = padded[lead - offset : lead - offset + row_count].astype(jnp.float32)
        result = result + jnp.where(keep_tap, taps_part[offset][None] * window, 0.0)
    return result


def on_device(qkv, taps, rate, angle, residue, skip, gain, lengths):
    tok_rows = qkv.shape[0]
    channels = qkv.shape[2]
    group_count = rate.shape[0]
    group_width = channels // group_count
    mode_count = rate.shape[1]
    reach = taps.shape[0]
    span_count = tok_rows // SPAN
    device = lax.axis_index("ctx")
    anchor = device * tok_rows
    positions = anchor + jnp.arange(tok_rows, dtype=jnp.int32)
    genome_start = genome_begin(lengths, positions)
    before = passed_along(qkv[tok_rows - (reach - 1) :], "ctx", 1)
    padded = jnp.concatenate([before, qkv], axis=0)
    filtered = short_filter(padded, taps, positions, genome_start)
    query, product = lax.optimization_barrier((filtered[:, 0], filtered[:, 1] * filtered[:, 2]))
    leaving, stepping = pole_exits(rate, angle, SPAN)
    values = jnp.transpose(
        product.reshape(span_count, SPAN, group_count, group_width), (0, 2, 3, 1)
    )
    span_pos = positions.reshape(span_count, SPAN)
    span_begin = genome_start.reshape(span_count, SPAN)
    summary = jnp.zeros((2, mode_count, group_count, group_width), jnp.float32)
    freshes = []
    keepers = []
    span_index = 0
    fresh_state = fresh_terms(
        leaving, values[span_index], span_pos[span_index], span_begin[span_index]
    )
    keep_state = span_begin[span_index, -1] < span_pos[span_index, 0]
    summary = jnp.where(keep_state, complex_times(stepping[..., None], summary), 0.0) + fresh_state
    freshes.append(fresh_state)
    keepers.append(keep_state)
    device_count = lax.axis_size("ctx")
    reach = min(device_count, -(-(GENOME_MAX - 1) // tok_rows))
    starting = jnp.cumsum(lengths) - lengths

    def unbroken(first_row, last_row):
        hit = (starting >= first_row) & (starting <= last_row)
        return jnp.logical_not(jnp.any(hit))

    def widen(factor):
        return jnp.repeat(factor, group_width, axis=2)

    running = passed_along(summary, "ctx", 1)
    pole_inputs, running = lax.optimization_barrier(((rate, angle, residue), running))
    tables = pole_tables(*pole_inputs, SPAN)
    response = tables[0]
    inside = inside_terms(
        toeplitz(response), values[span_index], span_pos[span_index], span_begin[span_index]
    )
    insides = [lax.optimization_barrier(inside)]
    power = stepping
    distance = 1
    while distance < reach:
        earlier = passed_along(running, "ctx", distance)
        alive = unbroken(anchor - distance * tok_rows, anchor - 1)
        factor = power[..., None] * alive.astype(jnp.float32)
        running = running + complex_times(factor, earlier)
        power = complex_times(power, power)
        distance = distance * 2
    incoming = running
    span_index = 0
    entered = (span_begin[span_index] < span_pos[span_index, 0])[None, None, :]
    outputs = [insides[span_index] + jnp.where(entered, carried(tables[1], incoming), 0.0)]
    stacked = jnp.stack(outputs, axis=0)
    long_part = jnp.transpose(stacked, (0, 3, 1, 2)).reshape(tok_rows, channels)
    gated_rows = query * (long_part + skip[None] * product)
    partial = jnp.sum(gated_rows * gated_rows, axis=1)
    squares = partial
    span = 1
    while span < lax.axis_size("tp"):
        pairs = [(i, i ^ span) for i in range(lax.axis_size("tp"))]
        squares = squares + lax.ppermute(squares, "tp", pairs)
        span = span * 2
    root_mean = jnp.sqrt(squares / D + EPSILON)
    return (gated_rows / root_mean[:, None] * gain[None]).astype(jnp.bfloat16)


def solution(mesh):
    return jax.shard_map(
        on_device,
        mesh=mesh,
        in_specs=(
            P("ctx", None, "tp"),
            P(None, None, "tp"),
            P("tp", None),
            P("tp", None),
            P(None, "tp", None),
            P("tp"),
            P("tp"),
            P(),
        ),
        out_specs=P("ctx", "tp"),
        check_vma=False,
    )
```

```python
import jax
import jax.numpy as jnp
from jax import lax
from jax.sharding import PartitionSpec as P

D = 8192
SPAN = 128
GENOME_MAX = 4096
X_RING = 4


HIGHEST = lax.Precision.HIGHEST
HIGH = lax.Precision.HIGH
EPSILON = 1e-06


def passed_along(block, axis, distance):
    devices = range(lax.axis_size(axis))
    route = [(i - distance, i) for i in devices if i - distance in devices]
    return lax.ppermute(block, axis, route)


def genome_begin(lengths, positions):
    ending = jnp.cumsum(lengths)
    starting = ending - lengths
    reached = starting[None, :] <= positions[:, None]
    return jnp.max(jnp.where(reached, starting[None, :], 0), axis=1)


def toeplitz(response):
    group_count, block = response.shape
    lag = jnp.arange(block, dtype=jnp.int32)
    picks = (lag[:, None, None] == lag[None, :, None] - lag[None, None, :]).astype(jnp.float32)
    return jnp.einsum("gk,kts->gts", response, picks, precision=HIGHEST)


def pole_tables(rate, angle, residue, block):
    counter = jnp.arange(block + 1).astype(jnp.float32)
    magnitude = jnp.exp(-rate[:, :, None] * counter)
    power_re = magnitude * jnp.cos(angle[:, :, None] * counter)
    power_im = magnitude * jnp.sin(angle[:, :, None] * counter)
    resid_re = residue[0][:, :, None]
    resid_im = residue[1][:, :, None]
    response = jnp.sum(
        resid_re * power_re[:, :, :block] - resid_im * power_im[:, :, :block], axis=1
    )
    enter_re = resid_re * power_re[:, :, 1:] - resid_im * power_im[:, :, 1:]
    enter_im = resid_re * power_im[:, :, 1:] + resid_im * power_re[:, :, 1:]
    entering = jnp.stack([enter_re, -enter_im])
    leaving = jnp.stack([power_re[:, :, block - 1 :: -1], power_im[:, :, block - 1 :: -1]])
    stepping = jnp.stack([power_re[:, :, block].T, power_im[:, :, block].T])
    return (response, entering, leaving, stepping)


def pole_exits(rate, angle, block):
    counter = (block - 1 - jnp.arange(block)).astype(jnp.float32)
    magnitude = jnp.exp(-rate[:, :, None] * counter)
    leaving = jnp.stack(
        [magnitude * jnp.cos(angle[:, :, None] * counter), magnitude * jnp.sin(angle[:, :, None] * counter)]
    )
    last = jnp.float32(block)
    step_size = jnp.exp(-rate * last)
    stepping = jnp.stack([(step_size * jnp.cos(angle * last)).T, (step_size * jnp.sin(angle * last)).T])
    return (leaving, stepping)


def complex_times(factor_one, factor_two):
    return jnp.stack(
        [
            factor_one[0] * factor_two[0] - factor_one[1] * factor_two[1],
            factor_one[0] * factor_two[1] + factor_one[1] * factor_two[0],
        ]
    )


def inside_terms(matrix_table, columns, block_positions, block_starts):
    same_genome = (block_positions[None, :] >= block_starts[:, None]).astype(jnp.float32)
    return jnp.einsum("gts,gis->git", matrix_table * same_genome[None], columns, precision=HIGH)


def fresh_terms(leaving, columns, block_positions, block_starts):
    tail_mask = (block_positions >= block_starts[-1]).astype(jnp.float32)
    return jnp.einsum("rgns,gis->rngi", leaving * tail_mask, columns, precision=HIGH)


def carried(entering, carry_state):
    return jnp.einsum("rgnt,rngi->git", entering, carry_state, precision=HIGH)


def short_filter(padded, taps_part, positions, genome_start):
    lead = taps_part.shape[0] - 1
    row_count = positions.shape[0]
    result = jnp.zeros((row_count,) + padded.shape[1:], jnp.float32)
    for offset in range(taps_part.shape[0]):
        keep_tap = (positions - offset >= genome_start)[:, None, None]
        window = padded[lead - offset : lead - offset + row_count].astype(jnp.float32)
        result = result + jnp.where(keep_tap, taps_part[offset][None] * window, 0.0)
    return result


def on_device(qkv, taps, rate, angle, residue, skip, gain, lengths):
    tok_rows = qkv.shape[0]
    channels = qkv.shape[2]
    group_count = rate.shape[0]
    group_width = channels // group_count
    mode_count = rate.shape[1]
    reach = taps.shape[0]
    span_count = tok_rows // SPAN
    device = lax.axis_index("ctx")
    anchor = device * tok_rows
    positions = anchor + jnp.arange(tok_rows, dtype=jnp.int32)
    genome_start = genome_begin(lengths, positions)
    before = passed_along(qkv[tok_rows - (reach - 1) :], "ctx", 1)
    padded = jnp.concatenate([before, qkv], axis=0)
    filtered = short_filter(padded, taps, positions, genome_start)
    query, product = lax.optimization_barrier((filtered[:, 0], filtered[:, 1] * filtered[:, 2]))
    leaving, stepping = pole_exits(rate, angle, SPAN)
    values = jnp.transpose(
        product.reshape(span_count, SPAN, group_count, group_width), (0, 2, 3, 1)
    )
    span_pos = positions.reshape(span_count, SPAN)
    span_begin = genome_start.reshape(span_count, SPAN)
    summary = jnp.zeros((2, mode_count, group_count, group_width), jnp.float32)
    freshes = []
    keepers = []
    span_index = 0
    fresh_state = fresh_terms(
        leaving, values[span_index], span_pos[span_index], span_begin[span_index]
    )
    keep_state = span_begin[span_index, -1] < span_pos[span_index, 0]
    summary = fresh_state
    freshes.append(fresh_state)
    keepers.append(keep_state)
    device_count = lax.axis_size("ctx")
    reach = min(device_count, -(-(GENOME_MAX - 1) // tok_rows))
    starting = jnp.cumsum(lengths) - lengths

    def unbroken(first_row, last_row):
        hit = (starting >= first_row) & (starting <= last_row)
        return jnp.logical_not(jnp.any(hit))

    def widen(factor):
        return jnp.repeat(factor, group_width, axis=2)

    running = passed_along(summary.reshape(2, mode_count, channels), "ctx", 1)
    pole_inputs, running = lax.optimization_barrier(((rate, angle, residue), running))
    tables = pole_tables(*pole_inputs, SPAN)
    response = tables[0]
    inside = inside_terms(
        toeplitz(response), values[span_index], span_pos[span_index], span_begin[span_index]
    )
    insides = [lax.optimization_barrier(inside)]
    power = stepping
    distance = 1
    while distance < reach:
        earlier = passed_along(running, "ctx", distance)
        alive = unbroken(anchor - distance * tok_rows, anchor - 1)
        factor = widen(power) * alive.astype(jnp.float32)
        running = running + complex_times(factor, earlier)
        power = complex_times(power, power)
        distance = distance * 2
    incoming = running.reshape(2, mode_count, group_count, group_width)
    span_index = 0
    entered = (span_begin[span_index] < span_pos[span_index, 0])[None, None, :]
    outputs = [insides[span_index] + jnp.where(entered, carried(tables[1], incoming), 0.0)]
    stacked = jnp.stack(outputs, axis=0)
    long_part = jnp.transpose(stacked, (0, 3, 1, 2)).reshape(tok_rows, channels)
    gated_rows = query * (long_part + skip[None] * product)
    partial = jnp.sum(gated_rows * gated_rows, axis=1)
    tp_count = lax.axis_size("tp")
    ring = X_RING if tp_count % X_RING == 0 else 1
    column = lax.axis_index("tp") % ring
    gathered = [partial]
    for offset in range(1, ring):
        pairs = [(i, i - i % ring + (i + offset) % ring) for i in range(tp_count)]
        gathered.append(lax.ppermute(partial, "tp", pairs))
    gathered = jnp.stack(gathered)
    squares = gathered[(column - 0) % ring]
    for source in range(1, ring):
        squares = squares + gathered[(column - source) % ring]
    span = ring
    while span < tp_count:
        pairs = [(i, i ^ span) for i in range(tp_count)]
        squares = squares + lax.ppermute(squares, "tp", pairs)
        span = span * 2
    root_mean = jnp.sqrt(squares / D + EPSILON)
    return (gated_rows / root_mean[:, None] * gain[None]).astype(jnp.bfloat16)


def solution(mesh):
    return jax.shard_map(
        on_device,
        mesh=mesh,
        in_specs=(
            P("ctx", None, "tp"),
            P(None, None, "tp"),
            P("tp", None),
            P("tp", None),
            P(None, "tp", None),
            P("tp"),
            P("tp"),
            P(),
        ),
        out_specs=P("ctx", "tp"),
        check_vma=False,
    )
```

```python
import jax
import jax.numpy as jnp
from jax import lax
from jax.sharding import PartitionSpec as P

D = 8192
SPAN = 128
GENOME_MAX = 4096
X_RING = 4


HIGHEST = lax.Precision.HIGHEST
HIGH = lax.Precision.HIGH
EPSILON = 1e-06


def passed_along(block, axis, distance):
    devices = range(lax.axis_size(axis))
    route = [(i - distance, i) for i in devices if i - distance in devices]
    return lax.ppermute(block, axis, route)


def genome_begin(lengths, positions):
    ending = jnp.cumsum(lengths)
    starting = ending - lengths
    reached = starting[None, :] <= positions[:, None]
    return jnp.max(jnp.where(reached, starting[None, :], 0), axis=1)


def toeplitz(response):
    group_count, block = response.shape
    lag = jnp.arange(block, dtype=jnp.int32)
    picks = (lag[:, None, None] == lag[None, :, None] - lag[None, None, :]).astype(jnp.float32)
    return jnp.einsum("gk,kts->gts", response, picks, precision=HIGHEST)


def pole_tables(rate, angle, residue, block):
    counter = jnp.arange(block + 1).astype(jnp.float32)
    magnitude = jnp.exp(-rate[:, :, None] * counter)
    power_re = magnitude * jnp.cos(angle[:, :, None] * counter)
    power_im = magnitude * jnp.sin(angle[:, :, None] * counter)
    resid_re = residue[0][:, :, None]
    resid_im = residue[1][:, :, None]
    response = jnp.sum(
        resid_re * power_re[:, :, :block] - resid_im * power_im[:, :, :block], axis=1
    )
    enter_re = resid_re * power_re[:, :, 1:] - resid_im * power_im[:, :, 1:]
    enter_im = resid_re * power_im[:, :, 1:] + resid_im * power_re[:, :, 1:]
    entering = jnp.stack([enter_re, -enter_im])
    leaving = jnp.stack([power_re[:, :, block - 1 :: -1], power_im[:, :, block - 1 :: -1]])
    stepping = jnp.stack([power_re[:, :, block].T, power_im[:, :, block].T])
    return (response, entering, leaving, stepping)


def pole_exits(rate, angle, block):
    counter = (block - 1 - jnp.arange(block)).astype(jnp.float32)
    magnitude = jnp.exp(-rate[:, :, None] * counter)
    leaving = jnp.stack(
        [magnitude * jnp.cos(angle[:, :, None] * counter), magnitude * jnp.sin(angle[:, :, None] * counter)]
    )
    last = jnp.float32(block)
    step_size = jnp.exp(-rate * last)
    stepping = jnp.stack([(step_size * jnp.cos(angle * last)).T, (step_size * jnp.sin(angle * last)).T])
    return (leaving, stepping)


def complex_times(factor_one, factor_two):
    return jnp.stack(
        [
            factor_one[0] * factor_two[0] - factor_one[1] * factor_two[1],
            factor_one[0] * factor_two[1] + factor_one[1] * factor_two[0],
        ]
    )


def inside_terms(matrix_table, columns, block_positions, block_starts):
    same_genome = (block_positions[None, :] >= block_starts[:, None]).astype(jnp.float32)
    return jnp.einsum("gts,gis->git", matrix_table * same_genome[None], columns, precision=HIGH)


def fresh_terms(leaving, columns, block_positions, block_starts):
    tail_mask = (block_positions >= block_starts[-1]).astype(jnp.float32)
    return jnp.einsum("rgns,gis->rngi", leaving * tail_mask, columns, precision=HIGH)


def carried(entering, carry_state):
    return jnp.einsum("rgnt,rngi->git", entering, carry_state, precision=HIGH)


def short_filter(padded, taps_part, positions, genome_start):
    lead = taps_part.shape[0] - 1
    row_count = positions.shape[0]
    result = jnp.zeros((row_count,) + padded.shape[1:], jnp.float32)
    for offset in range(taps_part.shape[0]):
        keep_tap = (positions - offset >= genome_start)[:, None, None]
        window = padded[lead - offset : lead - offset + row_count].astype(jnp.float32)
        result = result + jnp.where(keep_tap, taps_part[offset][None] * window, 0.0)
    return result


def on_device(qkv, taps, rate, angle, residue, skip, gain, lengths):
    tok_rows = qkv.shape[0]
    channels = qkv.shape[2]
    group_count = rate.shape[0]
    group_width = channels // group_count
    mode_count = rate.shape[1]
    reach = taps.shape[0]
    span_count = tok_rows // SPAN
    device = lax.axis_index("ctx")
    anchor = device * tok_rows
    positions = anchor + jnp.arange(tok_rows, dtype=jnp.int32)
    genome_start = genome_begin(lengths, positions)
    before = passed_along(qkv[tok_rows - (reach - 1) :], "ctx", 1)
    padded = jnp.concatenate([before, qkv], axis=0)
    filtered = short_filter(padded, taps, positions, genome_start)
    query, product = lax.optimization_barrier((filtered[:, 0], filtered[:, 1] * filtered[:, 2]))
    leaving, stepping = pole_exits(rate, angle, SPAN)
    values = jnp.transpose(
        product.reshape(span_count, SPAN, group_count, group_width), (0, 2, 3, 1)
    )
    span_pos = positions.reshape(span_count, SPAN)
    span_begin = genome_start.reshape(span_count, SPAN)
    summary = jnp.zeros((2, mode_count, group_count, group_width), jnp.float32)
    freshes = []
    keepers = []
    span_index = 0
    fresh_state = fresh_terms(
        leaving, values[span_index], span_pos[span_index], span_begin[span_index]
    )
    keep_state = span_begin[span_index, -1] < span_pos[span_index, 0]
    summary = fresh_state
    freshes.append(fresh_state)
    keepers.append(keep_state)
    device_count = lax.axis_size("ctx")
    reach = min(device_count, -(-(GENOME_MAX - 1) // tok_rows))
    starting = jnp.cumsum(lengths) - lengths

    def unbroken(first_row, last_row):
        hit = (starting >= first_row) & (starting <= last_row)
        return jnp.logical_not(jnp.any(hit))

    def widen(factor):
        return jnp.repeat(factor, group_width, axis=2)

    running = passed_along(summary, "ctx", 1)
    pole_inputs, running = lax.optimization_barrier(((rate, angle, residue), running))
    tables = pole_tables(*pole_inputs, SPAN)
    response = tables[0]
    inside = inside_terms(
        toeplitz(response), values[span_index], span_pos[span_index], span_begin[span_index]
    )
    insides = [lax.optimization_barrier(inside)]
    power = stepping
    distance = 1
    while distance < reach:
        earlier = passed_along(running, "ctx", distance)
        alive = unbroken(anchor - distance * tok_rows, anchor - 1)
        factor = power[..., None] * alive.astype(jnp.float32)
        running = running + complex_times(factor, earlier)
        power = complex_times(power, power)
        distance = distance * 2
    incoming = running
    span_index = 0
    entered = (span_begin[span_index] < span_pos[span_index, 0])[None, None, :]
    outputs = [insides[span_index] + jnp.where(entered, carried(tables[1], incoming), 0.0)]
    stacked = jnp.stack(outputs, axis=0)
    long_part = jnp.transpose(stacked, (0, 3, 1, 2)).reshape(tok_rows, channels)
    gated_rows = query * (long_part + skip[None] * product)
    partial = jnp.sum(gated_rows * gated_rows, axis=1)
    tp_count = lax.axis_size("tp")
    ring = X_RING if tp_count % X_RING == 0 else 1
    column = lax.axis_index("tp") % ring
    gathered = [partial]
    for offset in range(1, ring):
        pairs = [(i, i - i % ring + (i + offset) % ring) for i in range(tp_count)]
        gathered.append(lax.ppermute(partial, "tp", pairs))
    gathered = jnp.stack(gathered)
    squares = gathered[(column - 0) % ring]
    for source in range(1, ring):
        squares = squares + gathered[(column - source) % ring]
    span = ring
    while span < tp_count:
        pairs = [(i, i ^ span) for i in range(tp_count)]
        squares = squares + lax.ppermute(squares, "tp", pairs)
        span = span * 2
    root_mean = jnp.sqrt(squares / D + EPSILON)
    return (gated_rows / root_mean[:, None] * gain[None]).astype(jnp.bfloat16)


def solution(mesh):
    return jax.shard_map(
        on_device,
        mesh=mesh,
        in_specs=(
            P("ctx", None, "tp"),
            P(None, None, "tp"),
            P("tp", None),
            P("tp", None),
            P(None, "tp", None),
            P("tp"),
            P("tp"),
            P(),
        ),
        out_specs=P("ctx", "tp"),
        check_vma=False,
    )
```

```python
import jax
import jax.numpy as jnp
from jax import lax
from jax.sharding import PartitionSpec as P

D = 8192
SPAN = 128
GENOME_MAX = 4096
X_RING = 4


HIGHEST = lax.Precision.HIGHEST
HIGH = lax.Precision.HIGH
EPSILON = 1e-06


def passed_along(block, axis, distance):
    devices = range(lax.axis_size(axis))
    route = [(i - distance, i) for i in devices if i - distance in devices]
    return lax.ppermute(block, axis, route)


def genome_begin(lengths, positions):
    ending = jnp.cumsum(lengths)
    starting = ending - lengths
    reached = starting[None, :] <= positions[:, None]
    return jnp.max(jnp.where(reached, starting[None, :], 0), axis=1)


def toeplitz(response):
    group_count, block = response.shape
    lag = jnp.arange(block, dtype=jnp.int32)
    picks = (lag[:, None, None] == lag[None, :, None] - lag[None, None, :]).astype(jnp.float32)
    return jnp.einsum("gk,kts->gts", response, picks, precision=HIGHEST)


def pole_tables(rate, angle, residue, block):
    counter = jnp.arange(block + 1).astype(jnp.float32)
    magnitude = jnp.exp(-rate[:, :, None] * counter)
    power_re = magnitude * jnp.cos(angle[:, :, None] * counter)
    power_im = magnitude * jnp.sin(angle[:, :, None] * counter)
    resid_re = residue[0][:, :, None]
    resid_im = residue[1][:, :, None]
    response = jnp.sum(
        resid_re * power_re[:, :, :block] - resid_im * power_im[:, :, :block], axis=1
    )
    enter_re = resid_re * power_re[:, :, 1:] - resid_im * power_im[:, :, 1:]
    enter_im = resid_re * power_im[:, :, 1:] + resid_im * power_re[:, :, 1:]
    entering = jnp.stack([enter_re, -enter_im])
    leaving = jnp.stack([power_re[:, :, block - 1 :: -1], power_im[:, :, block - 1 :: -1]])
    stepping = jnp.stack([power_re[:, :, block].T, power_im[:, :, block].T])
    return (response, entering, leaving, stepping)


def pole_exits(rate, angle, block):
    counter = (block - 1 - jnp.arange(block)).astype(jnp.float32)
    magnitude = jnp.exp(-rate[:, :, None] * counter)
    leaving = jnp.stack(
        [magnitude * jnp.cos(angle[:, :, None] * counter), magnitude * jnp.sin(angle[:, :, None] * counter)]
    )
    last = jnp.float32(block)
    step_size = jnp.exp(-rate * last)
    stepping = jnp.stack([(step_size * jnp.cos(angle * last)).T, (step_size * jnp.sin(angle * last)).T])
    return (leaving, stepping)


def complex_times(factor_one, factor_two):
    return jnp.stack(
        [
            factor_one[0] * factor_two[0] - factor_one[1] * factor_two[1],
            factor_one[0] * factor_two[1] + factor_one[1] * factor_two[0],
        ]
    )


def inside_terms(matrix_table, columns, block_positions, block_starts):
    same_genome = (block_positions[None, :] >= block_starts[:, None]).astype(jnp.float32)
    return jnp.einsum("gts,gis->git", matrix_table * same_genome[None], columns, precision=HIGH)


def fresh_terms(leaving, columns, block_positions, block_starts):
    tail_mask = (block_positions >= block_starts[-1]).astype(jnp.float32)
    return jnp.einsum("rgns,gis->rngi", leaving * tail_mask, columns, precision=HIGH)


def carried(entering, carry_state):
    return jnp.einsum("rgnt,rngi->git", entering, carry_state, precision=HIGH)


def short_filter(padded, taps_part, positions, genome_start):
    lead = taps_part.shape[0] - 1
    row_count = positions.shape[0]
    result = jnp.zeros((row_count,) + padded.shape[1:], jnp.float32)
    for offset in range(taps_part.shape[0]):
        keep_tap = (positions - offset >= genome_start)[:, None, None]
        window = padded[lead - offset : lead - offset + row_count].astype(jnp.float32)
        result = result + jnp.where(keep_tap, taps_part[offset][None] * window, 0.0)
    return result


def on_device(qkv, taps, rate, angle, residue, skip, gain, lengths):
    tok_rows = qkv.shape[0]
    channels = qkv.shape[2]
    group_count = rate.shape[0]
    group_width = channels // group_count
    mode_count = rate.shape[1]
    reach = taps.shape[0]
    span_count = tok_rows // SPAN
    device = lax.axis_index("ctx")
    anchor = device * tok_rows
    positions = anchor + jnp.arange(tok_rows, dtype=jnp.int32)
    genome_start = genome_begin(lengths, positions)
    before = passed_along(qkv[tok_rows - (reach - 1) :], "ctx", 1)
    padded = jnp.concatenate([before, qkv], axis=0)
    filtered = short_filter(padded, taps, positions, genome_start)
    query, product = lax.optimization_barrier((filtered[:, 0], filtered[:, 1] * filtered[:, 2]))
    leaving, stepping = pole_exits(rate, angle, SPAN)
    values = jnp.transpose(
        product.reshape(span_count, SPAN, group_count, group_width), (0, 2, 3, 1)
    )
    span_pos = positions.reshape(span_count, SPAN)
    span_begin = genome_start.reshape(span_count, SPAN)
    summary = jnp.zeros((2, mode_count, group_count, group_width), jnp.float32)
    freshes = []
    keepers = []
    span_index = 0
    fresh_state = fresh_terms(
        leaving, values[span_index], span_pos[span_index], span_begin[span_index]
    )
    keep_state = span_begin[span_index, -1] < span_pos[span_index, 0]
    summary = fresh_state
    freshes.append(fresh_state)
    keepers.append(keep_state)
    device_count = lax.axis_size("ctx")
    reach = min(device_count, -(-(GENOME_MAX - 1) // tok_rows))
    starting = jnp.cumsum(lengths) - lengths

    def unbroken(first_row, last_row):
        hit = (starting >= first_row) & (starting <= last_row)
        return jnp.logical_not(jnp.any(hit))

    def widen(factor):
        return jnp.repeat(factor, group_width, axis=2)

    fresh = summary.reshape(2, mode_count, channels)
    running = passed_along(fresh, "ctx", 1)
    if reach > 1:
        older = passed_along(fresh, "ctx", 2)
        alive = unbroken(anchor - tok_rows, anchor - 1)
        running = running + complex_times(widen(stepping) * alive.astype(jnp.float32), older)
    pole_inputs, running = lax.optimization_barrier(((rate, angle, residue), running))
    tables = pole_tables(*pole_inputs, SPAN)
    response = tables[0]
    inside = inside_terms(
        toeplitz(response), values[span_index], span_pos[span_index], span_begin[span_index]
    )
    insides = [lax.optimization_barrier(inside)]
    power = complex_times(stepping, stepping)
    distance = 2
    while distance < reach:
        earlier = passed_along(running, "ctx", distance)
        alive = unbroken(anchor - distance * tok_rows, anchor - 1)
        factor = widen(power) * alive.astype(jnp.float32)
        running = running + complex_times(factor, earlier)
        power = complex_times(power, power)
        distance = distance * 2
    incoming = running.reshape(2, mode_count, group_count, group_width)
    span_index = 0
    entered = (span_begin[span_index] < span_pos[span_index, 0])[None, None, :]
    outputs = [insides[span_index] + jnp.where(entered, carried(tables[1], incoming), 0.0)]
    stacked = jnp.stack(outputs, axis=0)
    long_part = jnp.transpose(stacked, (0, 3, 1, 2)).reshape(tok_rows, channels)
    gated_rows = query * (long_part + skip[None] * product)
    partial = jnp.sum(gated_rows * gated_rows, axis=1)
    tp_count = lax.axis_size("tp")
    ring = X_RING if tp_count % X_RING == 0 else 1
    column = lax.axis_index("tp") % ring
    gathered = [partial]
    for offset in range(1, ring):
        pairs = [(i, i - i % ring + (i + offset) % ring) for i in range(tp_count)]
        gathered.append(lax.ppermute(partial, "tp", pairs))
    gathered = jnp.stack(gathered)
    squares = gathered[(column - 0) % ring]
    for source in range(1, ring):
        squares = squares + gathered[(column - source) % ring]
    span = ring
    while span < tp_count:
        pairs = [(i, i ^ span) for i in range(tp_count)]
        squares = squares + lax.ppermute(squares, "tp", pairs)
        span = span * 2
    root_mean = jnp.sqrt(squares / D + EPSILON)
    return (gated_rows / root_mean[:, None] * gain[None]).astype(jnp.bfloat16)


def solution(mesh):
    return jax.shard_map(
        on_device,
        mesh=mesh,
        in_specs=(
            P("ctx", None, "tp"),
            P(None, None, "tp"),
            P("tp", None),
            P("tp", None),
            P(None, "tp", None),
            P("tp"),
            P("tp"),
            P(),
        ),
        out_specs=P("ctx", "tp"),
        check_vma=False,
    )
```

```python
import jax
import jax.numpy as jnp
from jax import lax
from jax.sharding import PartitionSpec as P

D = 8192
SPAN = 128
GENOME_MAX = 4096
X_RING = 4


HIGHEST = lax.Precision.HIGHEST
HIGH = lax.Precision.HIGH
EPSILON = 1e-06


def passed_along(block, axis, distance):
    devices = range(lax.axis_size(axis))
    route = [(i - distance, i) for i in devices if i - distance in devices]
    return lax.ppermute(block, axis, route)


def genome_begin(lengths, positions):
    ending = jnp.cumsum(lengths)
    starting = ending - lengths
    reached = starting[None, :] <= positions[:, None]
    return jnp.max(jnp.where(reached, starting[None, :], 0), axis=1)


def toeplitz(response):
    group_count, block = response.shape
    lag = jnp.arange(block, dtype=jnp.int32)
    picks = (lag[:, None, None] == lag[None, :, None] - lag[None, None, :]).astype(jnp.float32)
    return jnp.einsum("gk,kts->gts", response, picks, precision=HIGHEST)


def pole_tables(rate, angle, residue, block):
    counter = jnp.arange(block + 1).astype(jnp.float32)
    magnitude = jnp.exp(-rate[:, :, None] * counter)
    power_re = magnitude * jnp.cos(angle[:, :, None] * counter)
    power_im = magnitude * jnp.sin(angle[:, :, None] * counter)
    resid_re = residue[0][:, :, None]
    resid_im = residue[1][:, :, None]
    response = jnp.sum(
        resid_re * power_re[:, :, :block] - resid_im * power_im[:, :, :block], axis=1
    )
    enter_re = resid_re * power_re[:, :, 1:] - resid_im * power_im[:, :, 1:]
    enter_im = resid_re * power_im[:, :, 1:] + resid_im * power_re[:, :, 1:]
    entering = jnp.stack([enter_re, -enter_im])
    leaving = jnp.stack([power_re[:, :, block - 1 :: -1], power_im[:, :, block - 1 :: -1]])
    stepping = jnp.stack([power_re[:, :, block].T, power_im[:, :, block].T])
    return (response, entering, leaving, stepping)


def pole_exits(rate, angle, block):
    counter = (block - 1 - jnp.arange(block)).astype(jnp.float32)
    magnitude = jnp.exp(-rate[:, :, None] * counter)
    leaving = jnp.stack(
        [magnitude * jnp.cos(angle[:, :, None] * counter), magnitude * jnp.sin(angle[:, :, None] * counter)]
    )
    last = jnp.float32(block)
    step_size = jnp.exp(-rate * last)
    stepping = jnp.stack([(step_size * jnp.cos(angle * last)).T, (step_size * jnp.sin(angle * last)).T])
    return (leaving, stepping)


def complex_times(factor_one, factor_two):
    return jnp.stack(
        [
            factor_one[0] * factor_two[0] - factor_one[1] * factor_two[1],
            factor_one[0] * factor_two[1] + factor_one[1] * factor_two[0],
        ]
    )


def inside_terms(matrix_table, columns, block_positions, block_starts):
    same_genome = (block_positions[None, :] >= block_starts[:, None]).astype(jnp.float32)
    return jnp.einsum("gts,gis->git", matrix_table * same_genome[None], columns, precision=HIGH)


def fresh_terms(leaving, columns, block_positions, block_starts):
    tail_mask = (block_positions >= block_starts[-1]).astype(jnp.float32)
    return jnp.einsum("rgns,gis->rngi", leaving * tail_mask, columns, precision=HIGH)


def carried(entering, carry_state):
    return jnp.einsum("rgnt,rngi->git", entering, carry_state, precision=HIGH)


def short_filter(padded, taps_part, positions, genome_start):
    lead = taps_part.shape[0] - 1
    row_count = positions.shape[0]
    result = jnp.zeros((row_count,) + padded.shape[1:], jnp.float32)
    for offset in range(taps_part.shape[0]):
        keep_tap = (positions - offset >= genome_start)[:, None, None]
        window = padded[lead - offset : lead - offset + row_count].astype(jnp.float32)
        result = result + jnp.where(keep_tap, taps_part[offset][None] * window, 0.0)
    return result


def on_device(qkv, taps, rate, angle, residue, skip, gain, lengths):
    tok_rows = qkv.shape[0]
    channels = qkv.shape[2]
    group_count = rate.shape[0]
    group_width = channels // group_count
    mode_count = rate.shape[1]
    reach = taps.shape[0]
    span_count = tok_rows // SPAN
    device = lax.axis_index("ctx")
    anchor = device * tok_rows
    positions = anchor + jnp.arange(tok_rows, dtype=jnp.int32)
    genome_start = genome_begin(lengths, positions)
    before = passed_along(qkv[tok_rows - (reach - 1) :], "ctx", 1)
    padded = jnp.concatenate([before, qkv], axis=0)
    filtered = short_filter(padded, taps, positions, genome_start)
    query, product = lax.optimization_barrier((filtered[:, 0], filtered[:, 1] * filtered[:, 2]))
    leaving, stepping = pole_exits(rate, angle, SPAN)
    values = jnp.transpose(
        product.reshape(span_count, SPAN, group_count, group_width), (0, 2, 3, 1)
    )
    span_pos = positions.reshape(span_count, SPAN)
    span_begin = genome_start.reshape(span_count, SPAN)
    summary = jnp.zeros((2, mode_count, group_count, group_width), jnp.float32)
    freshes = []
    keepers = []
    span_index = 0
    fresh_state = fresh_terms(
        leaving, values[span_index], span_pos[span_index], span_begin[span_index]
    )
    keep_state = span_begin[span_index, -1] < span_pos[span_index, 0]
    summary = fresh_state
    freshes.append(fresh_state)
    keepers.append(keep_state)
    device_count = lax.axis_size("ctx")
    reach = min(device_count, -(-(GENOME_MAX - 1) // tok_rows))
    starting = jnp.cumsum(lengths) - lengths

    def unbroken(first_row, last_row):
        hit = (starting >= first_row) & (starting <= last_row)
        return jnp.logical_not(jnp.any(hit))

    def widen(factor):
        return jnp.repeat(factor, group_width, axis=2)

    fresh = summary.reshape(2, mode_count, channels)
    running = passed_along(fresh, "ctx", 1)
    first_width = min(4, reach)
    power = stepping
    for distance in range(2, first_width + 1):
        older = passed_along(fresh, "ctx", distance)
        alive = unbroken(anchor - (distance - 1) * tok_rows, anchor - 1)
        running = running + complex_times(widen(power) * alive.astype(jnp.float32), older)
        power = complex_times(power, stepping)
    pole_inputs, running = lax.optimization_barrier(((rate, angle, residue), running))
    tables = pole_tables(*pole_inputs, SPAN)
    response = tables[0]
    inside = inside_terms(
        toeplitz(response), values[span_index], span_pos[span_index], span_begin[span_index]
    )
    insides = [lax.optimization_barrier(inside)]
    distance = first_width
    while distance < reach:
        earlier = passed_along(running, "ctx", distance)
        alive = unbroken(anchor - distance * tok_rows, anchor - 1)
        factor = widen(power) * alive.astype(jnp.float32)
        running = running + complex_times(factor, earlier)
        power = complex_times(power, power)
        distance = distance * 2
    incoming = running.reshape(2, mode_count, group_count, group_width)
    span_index = 0
    entered = (span_begin[span_index] < span_pos[span_index, 0])[None, None, :]
    outputs = [insides[span_index] + jnp.where(entered, carried(tables[1], incoming), 0.0)]
    stacked = jnp.stack(outputs, axis=0)
    long_part = jnp.transpose(stacked, (0, 3, 1, 2)).reshape(tok_rows, channels)
    gated_rows = query * (long_part + skip[None] * product)
    partial = jnp.sum(gated_rows * gated_rows, axis=1)
    tp_count = lax.axis_size("tp")
    ring = X_RING if tp_count % X_RING == 0 else 1
    column = lax.axis_index("tp") % ring
    gathered = [partial]
    for offset in range(1, ring):
        pairs = [(i, i - i % ring + (i + offset) % ring) for i in range(tp_count)]
        gathered.append(lax.ppermute(partial, "tp", pairs))
    gathered = jnp.stack(gathered)
    squares = gathered[(column - 0) % ring]
    for source in range(1, ring):
        squares = squares + gathered[(column - source) % ring]
    span = ring
    while span < tp_count:
        pairs = [(i, i ^ span) for i in range(tp_count)]
        squares = squares + lax.ppermute(squares, "tp", pairs)
        span = span * 2
    root_mean = jnp.sqrt(squares / D + EPSILON)
    return (gated_rows / root_mean[:, None] * gain[None]).astype(jnp.bfloat16)


def solution(mesh):
    return jax.shard_map(
        on_device,
        mesh=mesh,
        in_specs=(
            P("ctx", None, "tp"),
            P(None, None, "tp"),
            P("tp", None),
            P("tp", None),
            P(None, "tp", None),
            P("tp"),
            P("tp"),
            P(),
        ),
        out_specs=P("ctx", "tp"),
        check_vma=False,
    )
```

```python
import jax
import jax.numpy as jnp
from jax import lax
from jax.sharding import PartitionSpec as P

D = 8192
SPAN = 128
GENOME_MAX = 4096
X_RING = 4


HIGHEST = lax.Precision.HIGHEST
HIGH = lax.Precision.HIGH
EPSILON = 1e-06


def passed_along(block, axis, distance):
    devices = range(lax.axis_size(axis))
    route = [(i - distance, i) for i in devices if i - distance in devices]
    return lax.ppermute(block, axis, route)


def genome_begin(lengths, positions):
    ending = jnp.cumsum(lengths)
    starting = ending - lengths
    reached = starting[None, :] <= positions[:, None]
    return jnp.max(jnp.where(reached, starting[None, :], 0), axis=1)


def toeplitz(response):
    group_count, block = response.shape
    lag = jnp.arange(block, dtype=jnp.int32)
    picks = (lag[:, None, None] == lag[None, :, None] - lag[None, None, :]).astype(jnp.float32)
    return jnp.einsum("gk,kts->gts", response, picks, precision=HIGHEST)


def pole_tables(rate, angle, residue, block):
    counter = jnp.arange(block + 1).astype(jnp.float32)
    magnitude = jnp.exp(-rate[:, :, None] * counter)
    power_re = magnitude * jnp.cos(angle[:, :, None] * counter)
    power_im = magnitude * jnp.sin(angle[:, :, None] * counter)
    resid_re = residue[0][:, :, None]
    resid_im = residue[1][:, :, None]
    response = jnp.sum(
        resid_re * power_re[:, :, :block] - resid_im * power_im[:, :, :block], axis=1
    )
    enter_re = resid_re * power_re[:, :, 1:] - resid_im * power_im[:, :, 1:]
    enter_im = resid_re * power_im[:, :, 1:] + resid_im * power_re[:, :, 1:]
    entering = jnp.stack([enter_re, -enter_im])
    leaving = jnp.stack([power_re[:, :, block - 1 :: -1], power_im[:, :, block - 1 :: -1]])
    stepping = jnp.stack([power_re[:, :, block].T, power_im[:, :, block].T])
    return (response, entering, leaving, stepping)


def pole_exits(rate, angle, block):
    counter = (block - 1 - jnp.arange(block)).astype(jnp.float32)
    magnitude = jnp.exp(-rate[:, :, None] * counter)
    leaving = jnp.stack(
        [magnitude * jnp.cos(angle[:, :, None] * counter), magnitude * jnp.sin(angle[:, :, None] * counter)]
    )
    last = jnp.float32(block)
    step_size = jnp.exp(-rate * last)
    stepping = jnp.stack([(step_size * jnp.cos(angle * last)).T, (step_size * jnp.sin(angle * last)).T])
    return (leaving, stepping)


def complex_times(factor_one, factor_two):
    return jnp.stack(
        [
            factor_one[0] * factor_two[0] - factor_one[1] * factor_two[1],
            factor_one[0] * factor_two[1] + factor_one[1] * factor_two[0],
        ]
    )


def inside_terms(matrix_table, columns, block_positions, block_starts):
    same_genome = (block_positions[None, :] >= block_starts[:, None]).astype(jnp.float32)
    return jnp.einsum("gts,gis->git", matrix_table * same_genome[None], columns, precision=HIGH)


def fresh_terms(leaving, columns, block_positions, block_starts):
    tail_mask = (block_positions >= block_starts[-1]).astype(jnp.float32)
    return jnp.einsum("rgns,gis->rngi", leaving * tail_mask, columns, precision=HIGH)


def carried(entering, carry_state):
    return jnp.einsum("rgnt,rngi->git", entering, carry_state, precision=HIGH)


def short_filter(padded, taps_part, positions, genome_start):
    lead = taps_part.shape[0] - 1
    row_count = positions.shape[0]
    result = jnp.zeros((row_count,) + padded.shape[1:], jnp.float32)
    for offset in range(taps_part.shape[0]):
        keep_tap = (positions - offset >= genome_start)[:, None, None]
        window = padded[lead - offset : lead - offset + row_count].astype(jnp.float32)
        result = result + jnp.where(keep_tap, taps_part[offset][None] * window, 0.0)
    return result


def on_device(qkv, taps, rate, angle, residue, skip, gain, lengths):
    tok_rows = qkv.shape[0]
    channels = qkv.shape[2]
    group_count = rate.shape[0]
    group_width = channels // group_count
    mode_count = rate.shape[1]
    reach = taps.shape[0]
    span_count = tok_rows // SPAN
    device = lax.axis_index("ctx")
    anchor = device * tok_rows
    positions = anchor + jnp.arange(tok_rows, dtype=jnp.int32)
    genome_start = genome_begin(lengths, positions)
    before = passed_along(qkv[tok_rows - (reach - 1) :], "ctx", 1)
    padded = jnp.concatenate([before, qkv], axis=0)
    filtered = short_filter(padded, taps, positions, genome_start)
    query, product = lax.optimization_barrier((filtered[:, 0], filtered[:, 1] * filtered[:, 2]))
    leaving, stepping = pole_exits(rate, angle, SPAN)
    values = jnp.transpose(
        product.reshape(span_count, SPAN, group_count, group_width), (0, 2, 3, 1)
    )
    span_pos = positions.reshape(span_count, SPAN)
    span_begin = genome_start.reshape(span_count, SPAN)
    summary = jnp.zeros((2, mode_count, group_count, group_width), jnp.float32)
    freshes = []
    keepers = []
    span_index = 0
    fresh_state = fresh_terms(
        leaving, values[span_index], span_pos[span_index], span_begin[span_index]
    )
    keep_state = span_begin[span_index, -1] < span_pos[span_index, 0]
    summary = fresh_state
    freshes.append(fresh_state)
    keepers.append(keep_state)
    device_count = lax.axis_size("ctx")
    reach = min(device_count, -(-(GENOME_MAX - 1) // tok_rows))
    starting = jnp.cumsum(lengths) - lengths

    def unbroken(first_row, last_row):
        hit = (starting >= first_row) & (starting <= last_row)
        return jnp.logical_not(jnp.any(hit))

    def widen(factor):
        return jnp.repeat(factor, group_width, axis=2)

    fresh = summary.reshape(2, mode_count, channels)
    running = passed_along(fresh, "ctx", 1)
    first_width = min(8, reach)
    power = stepping
    for distance in range(2, first_width + 1):
        older = passed_along(fresh, "ctx", distance)
        alive = unbroken(anchor - (distance - 1) * tok_rows, anchor - 1)
        running = running + complex_times(widen(power) * alive.astype(jnp.float32), older)
        power = complex_times(power, stepping)
    pole_inputs, running = lax.optimization_barrier(((rate, angle, residue), running))
    tables = pole_tables(*pole_inputs, SPAN)
    response = tables[0]
    inside = inside_terms(
        toeplitz(response), values[span_index], span_pos[span_index], span_begin[span_index]
    )
    insides = [lax.optimization_barrier(inside)]
    distance = first_width
    while distance < reach:
        earlier = passed_along(running, "ctx", distance)
        alive = unbroken(anchor - distance * tok_rows, anchor - 1)
        factor = widen(power) * alive.astype(jnp.float32)
        running = running + complex_times(factor, earlier)
        power = complex_times(power, power)
        distance = distance * 2
    incoming = running.reshape(2, mode_count, group_count, group_width)
    span_index = 0
    entered = (span_begin[span_index] < span_pos[span_index, 0])[None, None, :]
    outputs = [insides[span_index] + jnp.where(entered, carried(tables[1], incoming), 0.0)]
    stacked = jnp.stack(outputs, axis=0)
    long_part = jnp.transpose(stacked, (0, 3, 1, 2)).reshape(tok_rows, channels)
    gated_rows = query * (long_part + skip[None] * product)
    partial = jnp.sum(gated_rows * gated_rows, axis=1)
    tp_count = lax.axis_size("tp")
    ring = X_RING if tp_count % X_RING == 0 else 1
    column = lax.axis_index("tp") % ring
    gathered = [partial]
    for offset in range(1, ring):
        pairs = [(i, i - i % ring + (i + offset) % ring) for i in range(tp_count)]
        gathered.append(lax.ppermute(partial, "tp", pairs))
    gathered = jnp.stack(gathered)
    squares = gathered[(column - 0) % ring]
    for source in range(1, ring):
        squares = squares + gathered[(column - source) % ring]
    span = ring
    while span < tp_count:
        pairs = [(i, i ^ span) for i in range(tp_count)]
        squares = squares + lax.ppermute(squares, "tp", pairs)
        span = span * 2
    root_mean = jnp.sqrt(squares / D + EPSILON)
    return (gated_rows / root_mean[:, None] * gain[None]).astype(jnp.bfloat16)


def solution(mesh):
    return jax.shard_map(
        on_device,
        mesh=mesh,
        in_specs=(
            P("ctx", None, "tp"),
            P(None, None, "tp"),
            P("tp", None),
            P("tp", None),
            P(None, "tp", None),
            P("tp"),
            P("tp"),
            P(),
        ),
        out_specs=P("ctx", "tp"),
        check_vma=False,
    )
```

```python
import jax
import jax.numpy as jnp
from jax import lax
from jax.sharding import PartitionSpec as P

D = 8192
SPAN = 128
GENOME_MAX = 4096
X_RING = 4


HIGHEST = lax.Precision.HIGHEST
HIGH = lax.Precision.HIGH
EPSILON = 1e-06


def passed_along(block, axis, distance):
    devices = range(lax.axis_size(axis))
    route = [(i - distance, i) for i in devices if i - distance in devices]
    return lax.ppermute(block, axis, route)


def genome_begin(lengths, positions):
    ending = jnp.cumsum(lengths)
    starting = ending - lengths
    reached = starting[None, :] <= positions[:, None]
    return jnp.max(jnp.where(reached, starting[None, :], 0), axis=1)


def toeplitz(response):
    group_count, block = response.shape
    lag = jnp.arange(block, dtype=jnp.int32)
    picks = (lag[:, None, None] == lag[None, :, None] - lag[None, None, :]).astype(jnp.float32)
    return jnp.einsum("gk,kts->gts", response, picks, precision=HIGH)


def pole_tables(rate, angle, residue, block):
    counter = jnp.arange(block + 1).astype(jnp.float32)
    magnitude = jnp.exp(-rate[:, :, None] * counter)
    power_re = magnitude * jnp.cos(angle[:, :, None] * counter)
    power_im = magnitude * jnp.sin(angle[:, :, None] * counter)
    resid_re = residue[0][:, :, None]
    resid_im = residue[1][:, :, None]
    response = jnp.sum(
        resid_re * power_re[:, :, :block] - resid_im * power_im[:, :, :block], axis=1
    )
    enter_re = resid_re * power_re[:, :, 1:] - resid_im * power_im[:, :, 1:]
    enter_im = resid_re * power_im[:, :, 1:] + resid_im * power_re[:, :, 1:]
    entering = jnp.stack([enter_re, -enter_im])
    leaving = jnp.stack([power_re[:, :, block - 1 :: -1], power_im[:, :, block - 1 :: -1]])
    stepping = jnp.stack([power_re[:, :, block].T, power_im[:, :, block].T])
    return (response, entering, leaving, stepping)


def pole_exits(rate, angle, block):
    counter = (block - 1 - jnp.arange(block)).astype(jnp.float32)
    magnitude = jnp.exp(-rate[:, :, None] * counter)
    leaving = jnp.stack(
        [magnitude * jnp.cos(angle[:, :, None] * counter), magnitude * jnp.sin(angle[:, :, None] * counter)]
    )
    last = jnp.float32(block)
    step_size = jnp.exp(-rate * last)
    stepping = jnp.stack([(step_size * jnp.cos(angle * last)).T, (step_size * jnp.sin(angle * last)).T])
    return (leaving, stepping)


def complex_times(factor_one, factor_two):
    return jnp.stack(
        [
            factor_one[0] * factor_two[0] - factor_one[1] * factor_two[1],
            factor_one[0] * factor_two[1] + factor_one[1] * factor_two[0],
        ]
    )


def inside_terms(matrix_table, columns, block_positions, block_starts):
    same_genome = (block_positions[None, :] >= block_starts[:, None]).astype(jnp.float32)
    return jnp.einsum("gts,gis->git", matrix_table * same_genome[None], columns, precision=HIGH)


def fresh_terms(leaving, columns, block_positions, block_starts):
    tail_mask = (block_positions >= block_starts[-1]).astype(jnp.float32)
    return jnp.einsum("rgns,gis->rngi", leaving * tail_mask, columns, precision=HIGH)


def carried(entering, carry_state):
    return jnp.einsum("rgnt,rngi->git", entering, carry_state, precision=HIGH)


def short_filter(padded, taps_part, positions, genome_start):
    lead = taps_part.shape[0] - 1
    row_count = positions.shape[0]
    result = jnp.zeros((row_count,) + padded.shape[1:], jnp.float32)
    for offset in range(taps_part.shape[0]):
        keep_tap = (positions - offset >= genome_start)[:, None, None]
        window = padded[lead - offset : lead - offset + row_count].astype(jnp.float32)
        result = result + jnp.where(keep_tap, taps_part[offset][None] * window, 0.0)
    return result


def on_device(qkv, taps, rate, angle, residue, skip, gain, lengths):
    tok_rows = qkv.shape[0]
    channels = qkv.shape[2]
    group_count = rate.shape[0]
    group_width = channels // group_count
    mode_count = rate.shape[1]
    reach = taps.shape[0]
    span_count = tok_rows // SPAN
    device = lax.axis_index("ctx")
    anchor = device * tok_rows
    positions = anchor + jnp.arange(tok_rows, dtype=jnp.int32)
    genome_start = genome_begin(lengths, positions)
    before = passed_along(qkv[tok_rows - (reach - 1) :], "ctx", 1)
    padded = jnp.concatenate([before, qkv], axis=0)
    filtered = short_filter(padded, taps, positions, genome_start)
    query, product = lax.optimization_barrier((filtered[:, 0], filtered[:, 1] * filtered[:, 2]))
    leaving, stepping = pole_exits(rate, angle, SPAN)
    values = jnp.transpose(
        product.reshape(span_count, SPAN, group_count, group_width), (0, 2, 3, 1)
    )
    span_pos = positions.reshape(span_count, SPAN)
    span_begin = genome_start.reshape(span_count, SPAN)
    summary = jnp.zeros((2, mode_count, group_count, group_width), jnp.float32)
    freshes = []
    keepers = []
    span_index = 0
    fresh_state = fresh_terms(
        leaving, values[span_index], span_pos[span_index], span_begin[span_index]
    )
    keep_state = span_begin[span_index, -1] < span_pos[span_index, 0]
    summary = fresh_state
    freshes.append(fresh_state)
    keepers.append(keep_state)
    device_count = lax.axis_size("ctx")
    reach = min(device_count, -(-(GENOME_MAX - 1) // tok_rows))
    starting = jnp.cumsum(lengths) - lengths

    def unbroken(first_row, last_row):
        hit = (starting >= first_row) & (starting <= last_row)
        return jnp.logical_not(jnp.any(hit))

    def widen(factor):
        return jnp.repeat(factor, group_width, axis=2)

    fresh = summary.reshape(2, mode_count, channels)
    running = passed_along(fresh, "ctx", 1)
    first_width = min(4, reach)
    power = stepping
    for distance in range(2, first_width + 1):
        older = passed_along(fresh, "ctx", distance)
        alive = unbroken(anchor - (distance - 1) * tok_rows, anchor - 1)
        running = running + complex_times(widen(power) * alive.astype(jnp.float32), older)
        power = complex_times(power, stepping)
    pole_inputs, running = lax.optimization_barrier(((rate, angle, residue), running))
    tables = pole_tables(*pole_inputs, SPAN)
    response = tables[0]
    inside = inside_terms(
        toeplitz(response), values[span_index], span_pos[span_index], span_begin[span_index]
    )
    insides = [lax.optimization_barrier(inside)]
    distance = first_width
    while distance < reach:
        earlier = passed_along(running, "ctx", distance)
        alive = unbroken(anchor - distance * tok_rows, anchor - 1)
        factor = widen(power) * alive.astype(jnp.float32)
        running = running + complex_times(factor, earlier)
        power = complex_times(power, power)
        distance = distance * 2
    incoming = running.reshape(2, mode_count, group_count, group_width)
    span_index = 0
    entered = (span_begin[span_index] < span_pos[span_index, 0])[None, None, :]
    outputs = [insides[span_index] + jnp.where(entered, carried(tables[1], incoming), 0.0)]
    stacked = jnp.stack(outputs, axis=0)
    long_part = jnp.transpose(stacked, (0, 3, 1, 2)).reshape(tok_rows, channels)
    gated_rows = query * (long_part + skip[None] * product)
    partial = jnp.sum(gated_rows * gated_rows, axis=1)
    tp_count = lax.axis_size("tp")
    ring = X_RING if tp_count % X_RING == 0 else 1
    column = lax.axis_index("tp") % ring
    gathered = [partial]
    for offset in range(1, ring):
        pairs = [(i, i - i % ring + (i + offset) % ring) for i in range(tp_count)]
        gathered.append(lax.ppermute(partial, "tp", pairs))
    gathered = jnp.stack(gathered)
    squares = gathered[(column - 0) % ring]
    for source in range(1, ring):
        squares = squares + gathered[(column - source) % ring]
    span = ring
    while span < tp_count:
        pairs = [(i, i ^ span) for i in range(tp_count)]
        squares = squares + lax.ppermute(squares, "tp", pairs)
        span = span * 2
    root_mean = jnp.sqrt(squares / D + EPSILON)
    return (gated_rows / root_mean[:, None] * gain[None]).astype(jnp.bfloat16)


def solution(mesh):
    return jax.shard_map(
        on_device,
        mesh=mesh,
        in_specs=(
            P("ctx", None, "tp"),
            P(None, None, "tp"),
            P("tp", None),
            P("tp", None),
            P(None, "tp", None),
            P("tp"),
            P("tp"),
            P(),
        ),
        out_specs=P("ctx", "tp"),
        check_vma=False,
    )
```
